128 devices in a mesh: ctx: 16 (over z, x), head: 8 (over y, core).
Axes of the slice: x: 4, y: 4, z: 4, core: 2. Of those that a mesh axis runs over, the one named last changes fastest.
Arguments:
- queries: bfloat16 [16384, 4096], P(('ctx', 'head')), may hold values from -15 to 15
- keys: bfloat16 [16384, 512], P(('ctx', 'head')), may hold values from -6 to 6
- values: bfloat16 [16384, 512], P(('ctx', 'head')), may hold values from -6 to 6
- out_weight: bfloat16 [4096, 4096], P(None, 'ctx'), may hold values from -0.09375 to 0.09375
- vertical: int32 [32, 8], replicated, may hold values from -1 to 127, as said below
- slash: int32 [32, 4], replicated, may hold values from -1 to 8, as said below
Outputs:
- layer_out: bfloat16 [16384, 4096], P(('ctx', 'head'))
The draws below stay inside these ranges and needn't reach their ends.
Inputs may be any that keep to these rules, and one draw needn't show every extreme that they name: `vertical`: row h holds distinct tiles, entry 0 is tile 0, live entries first and -1 after them, at least one live; one head has all 8 live, among them tile 128 - 1. `slash`: row h holds distinct offsets, live entries first and -1 after them, at least one live; one head has all 4 live, among them 8.
All inputs are finite; a program needn't handle non-finite values.
Results may differ from the reference program's by a relative error of at most 0.0052.
Values may be sent and summed in bfloat16 or wider, within the bound.
No kernel may reach another device: no remote copies, remote signals or barrier semaphores. Data moves between devices by JAX's collectives and lax.ppermute only.
A program may use at most 128 MiB of HBM per device.

```python
import jax
import jax.numpy as jnp
from jax import lax

D = 4096
QUERY_HEAD_COUNT = 32
KEY_VALUE_HEADS = 4
HEAD_SIZE = 128
TILE_TOKENS = 128
NV = 8
NSL = 4
SEQUENCE_TOKENS = 16384
NB = 128
QB_LOC = 8


def draw_queries(key, part):
    starting_key = jax.random.fold_in(key, 11)
    sampled_picks = jnp.clip(2.5 * jax.random.normal(starting_key, (SEQUENCE_TOKENS, QUERY_HEAD_COUNT, HEAD_SIZE), jnp.float32), -15.0, 15.0)
    return sampled_picks.reshape(SEQUENCE_TOKENS, QUERY_HEAD_COUNT * HEAD_SIZE).astype(jnp.bfloat16)


def draw_keys(key, part):
    starting_key = jax.random.fold_in(key, 13)
    sampled_picks = jnp.clip(jax.random.normal(starting_key, (SEQUENCE_TOKENS, KEY_VALUE_HEADS, HEAD_SIZE), jnp.float32), -6.0, 6.0)
    return sampled_picks.reshape(SEQUENCE_TOKENS, KEY_VALUE_HEADS * HEAD_SIZE).astype(jnp.bfloat16)


def list_counts(key):
    first_key, second_key, third_key, fourth_key = jax.random.split(jax.random.fold_in(key, 101), 4)
    head_ids = jnp.arange(QUERY_HEAD_COUNT, dtype=jnp.int32)
    vert_counts = jax.random.randint(first_key, (QUERY_HEAD_COUNT,), 1, NV + 1)
    slash_counts = jax.random.randint(second_key, (QUERY_HEAD_COUNT,), 1, NSL + 1)
    vert_full = jax.random.randint(third_key, (), 0, QUERY_HEAD_COUNT)
    slash_full = jax.random.randint(fourth_key, (), 0, QUERY_HEAD_COUNT)
    vert_counts = jnp.where(head_ids == vert_full, NV, vert_counts)
    slash_counts = jnp.where(head_ids == slash_full, NSL, slash_counts)
    return (vert_counts, slash_counts, vert_full, slash_full)


def draw_vertical(key, part):
    vert_counts, slash_counts, vert_full, slash_full = list_counts(key)
    head_keys = jax.random.split(jax.random.fold_in(key, 202), QUERY_HEAD_COUNT)
    picked = jax.vmap(lambda head_key: jax.random.permutation(head_key, NB - 2)[:NV - 1])(head_keys) + 1
    head_ids = jnp.arange(QUERY_HEAD_COUNT, dtype=jnp.int32)
    picked = jnp.where((head_ids == vert_full)[:, None] & (jnp.arange(NV - 1) == 0)[None, :], NB - 1, picked)
    listed = jnp.concatenate([jnp.zeros((QUERY_HEAD_COUNT, 1), jnp.int32), picked.astype(jnp.int32)], axis=1)
    return jnp.where(jnp.arange(NV)[None, :] < vert_counts[:, None], listed, -1).astype(jnp.int32)


def draw_slash(key, part):
    vert_counts, slash_counts, vert_full, slash_full = list_counts(key)
    head_keys = jax.random.split(jax.random.fold_in(key, 303), QUERY_HEAD_COUNT)
    picked = jax.vmap(lambda head_key: jax.random.permutation(head_key, QB_LOC)[:NSL])(head_keys) + 1
    highest = QB_LOC - jnp.arange(NSL, dtype=jnp.int32)
    head_ids = jnp.arange(QUERY_HEAD_COUNT, dtype=jnp.int32)
    picked = jnp.where((head_ids == slash_full)[:, None], highest[None, :], picked)
    return jnp.where(jnp.arange(NSL)[None, :] < slash_counts[:, None], picked, -1).astype(jnp.int32)


def steps_of(stream_key, dims, shards, smallest, high):
    loudness = 1.0
    for dim, parts in shards:
        steps = jax.random.uniform(jax.random.fold_in(jax.random.fold_in(stream_key, 6), dim), (parts,), jnp.float32, smallest / len(shards), high / len(shards))
        loudness = loudness * jnp.repeat(jnp.exp(steps), dims[dim] // parts).reshape((-1,) + (1,) * (len(dims) - 1 - dim))
    return loudness


def scatter_about(key, shape, scale, limit, cuts=(), kind=jnp.bfloat16):
    result = jax.random.normal(key, shape, jnp.float32) * scale
    if len(cuts) > 0:
        result = steps_of(key, shape, cuts, -0.22, 0.18) * result
    return jnp.clip(result, min=-limit, max=limit).astype(kind)


def setup_inputs(seed: int = 0) -> dict:
    streams_of = jax.random.split(jax.random.key(seed), 7)
    queries = draw_queries(jax.random.fold_in(streams_of[6], 71), 0)
    keys = draw_keys(jax.random.fold_in(streams_of[6], 71), 0)
    values = scatter_about(streams_of[2], (SEQUENCE_TOKENS, KEY_VALUE_HEADS * HEAD_SIZE), 1.0, 6.0, ((0, 128),))
    out_weight = scatter_about(streams_of[3], (QUERY_HEAD_COUNT * HEAD_SIZE, D), (QUERY_HEAD_COUNT * HEAD_SIZE) ** -0.5, 0.09375, ((1, 16),))
    vertical = draw_vertical(jax.random.fold_in(streams_of[6], 71), 0)
    slash = draw_slash(jax.random.fold_in(streams_of[6], 71), 0)
    return dict(queries=queries, keys=keys, values=values, out_weight=out_weight, vertical=vertical, slash=slash)


def reference(queries, keys, values, out_weight, vertical, slash):
    total_rows = queries.shape[0]
    block_amount_total = total_rows // TILE_TOKENS
    group_width = QUERY_HEAD_COUNT // KEY_VALUE_HEADS
    q_blocks = queries.reshape(block_amount_total, TILE_TOKENS, QUERY_HEAD_COUNT, HEAD_SIZE)
    key_blocks = keys.reshape(block_amount_total, TILE_TOKENS, KEY_VALUE_HEADS, HEAD_SIZE)
    value_blocks = values.reshape(block_amount_total, TILE_TOKENS, KEY_VALUE_HEADS, HEAD_SIZE)
    block_ids = jnp.arange(block_amount_total, dtype=jnp.int32)
    causal = jnp.tril(jnp.ones((TILE_TOKENS, TILE_TOKENS), dtype=bool))
    not_first = jnp.arange(1 + NSL + NV) > 0
    token_shape = not_first[None, None, :, None] | causal[None, :, None, :]

    def one_head(head_index):
        kv_index = head_index // group_width
        query_local = jnp.take(q_blocks, head_index, axis=2).astype(jnp.float32)
        k_here = jnp.take(key_blocks, kv_index, axis=2)
        v_here = jnp.take(value_blocks, kv_index, axis=2)
        slash_row = jnp.take(slash, head_index, axis=0)
        vert_row = jnp.take(vertical, head_index, axis=0)
        live_slash = slash_row >= 1
        slash_blocks = block_ids[:, None] - slash_row[None, :]
        slash_ok = live_slash[None, :] & (slash_blocks >= 0)
        repeats = jnp.any(((block_ids[:, None] - vert_row[None, :])[:, :, None] == slash_row[None, None, :]) & live_slash[None, None, :], axis=2)
        vert_ok = (vert_row[None, :] >= 0) & (vert_row[None, :] < block_ids[:, None]) & jnp.logical_not(repeats)
        cand_ids = jnp.concatenate([block_ids[:, None], slash_blocks, jnp.broadcast_to(vert_row[None, :], (block_amount_total, NV))], axis=1)
        cand_ok = jnp.concatenate([jnp.ones((block_amount_total, 1), dtype=bool), slash_ok, vert_ok], axis=1)
        cand_ids = jnp.clip(cand_ids, 0, block_amount_total - 1).astype(jnp.int32)
        key_selected = jnp.take(k_here, cand_ids, axis=0).astype(jnp.float32)
        value_selected = jnp.take(v_here, cand_ids, axis=0).astype(jnp.float32)
        logit_scores = jnp.einsum("jps,jiys->jpiy", query_local, key_selected, precision=lax.Precision.HIGHEST) * (HEAD_SIZE ** -0.5)
        allowed = cand_ok[:, None, :, None] & token_shape
        masked = jnp.where(allowed, logit_scores, -jnp.inf)
        row_top = jnp.max(masked, axis=(2, 3), keepdims=True)
        weights = jnp.exp(masked - row_top)
        row_sum_total = jnp.sum(weights, axis=(2, 3))
        probabilities = lax.optimization_barrier(weights.astype(jnp.bfloat16)).astype(jnp.float32)
        blended_rows = jnp.einsum("uvla,ulam->uvm", probabilities, value_selected, precision=lax.Precision.HIGHEST) / row_sum_total[:, :, None]
        return blended_rows.astype(jnp.bfloat16)

    per_head = lax.map(one_head, jnp.arange(QUERY_HEAD_COUNT, dtype=jnp.int32))
    attended = per_head.transpose(1, 2, 0, 3).reshape(total_rows, QUERY_HEAD_COUNT * HEAD_SIZE)
    return jnp.dot(attended, out_weight, preferred_element_type=jnp.float32).astype(jnp.bfloat16)
```

```python
import numpy as np
import jax
import jax.numpy as jnp
from jax import lax
from jax.sharding import Mesh, PartitionSpec as P

HEAD_SIZE = 128
TILE_TOKENS = 128
CTX_AXES = ("cz", "cx")


def passed_along(block, axes, distance):
    count = 1
    for axis in axes:
        count *= lax.axis_size(axis)
    route = [(i - distance, i) for i in range(count) if i - distance >= 0]
    return lax.ppermute(block, axes, route)


def shards(queries, keys, values, out_weight, vertical, slash):
    head_count = lax.axis_size("head")
    head_index = lax.axis_index("head")
    cx_count = lax.axis_size("cx")
    ctx_index = lax.axis_index("cz") * cx_count + lax.axis_index("cx")
    tok_rows = queries.shape[0]
    query_heads = vertical.shape[0]
    kv_count = keys.shape[1] // HEAD_SIZE
    group_width = query_heads // kv_count
    per_dev = query_heads // head_count
    ctx_rows = tok_rows * head_count
    block_count = ctx_rows // TILE_TOKENS
    slash_span = block_count
    band = slash_span + 1

    kv_of_dest = (np.arange(head_count) * per_dev) // group_width
    q_part = queries.reshape(tok_rows, head_count, per_dev * HEAD_SIZE)
    k_part = jnp.take(keys.reshape(tok_rows, kv_count, HEAD_SIZE), kv_of_dest, axis=1)
    v_part = jnp.take(values.reshape(tok_rows, kv_count, HEAD_SIZE), kv_of_dest, axis=1)
    send = jnp.concatenate([q_part, k_part, v_part], axis=2).reshape(tok_rows, -1)
    recv = lax.all_to_all(send, "head", split_axis=1, concat_axis=0, tiled=True)
    q_width = per_dev * HEAD_SIZE
    q_loc = recv[:, :q_width]
    kv_loc = recv[:, q_width:]
    kv_prev = passed_along(kv_loc, CTX_AXES, 1)
    wide = jnp.concatenate([kv_prev, kv_loc], axis=0)

    my_heads = head_index * per_dev + jnp.arange(per_dev, dtype=jnp.int32)
    my_vertical = jnp.take(vertical, my_heads, axis=0)
    my_slash = jnp.take(slash, my_heads, axis=0)
    first_block = ctx_index * block_count
    local_vertical = my_vertical - first_block
    inside = (my_vertical >= 0) & (local_vertical >= 0) & (local_vertical < block_count)
    vertical_index = jnp.clip(local_vertical, 0, block_count - 1)
    kv_blocks = kv_loc.reshape(block_count, TILE_TOKENS, 2 * HEAD_SIZE)
    found = jnp.take(kv_blocks, vertical_index, axis=0)
    found = jnp.where(inside[:, :, None, None], found, jnp.zeros((), found.dtype))
    vertical_kv = lax.psum(found, CTX_AXES)
    vert_k = vertical_kv[..., :HEAD_SIZE]
    vert_v = vertical_kv[..., HEAD_SIZE:]

    band_kv = jnp.stack(
        [
            lax.slice_in_dim(
                wide, (b + block_count - slash_span) * TILE_TOKENS,
                (b + block_count + 1) * TILE_TOKENS, axis=0,
            )
            for b in range(block_count)
        ]
    )
    band_k = band_kv[..., :HEAD_SIZE]
    band_v = band_kv[..., HEAD_SIZE:]
    q_b = q_loc.reshape(block_count, TILE_TOKENS, per_dev, HEAD_SIZE)
    score_scale = HEAD_SIZE ** (-0.5)

    block_ids = first_block + jnp.arange(block_count, dtype=jnp.int32)
    offsets = slash_span - jnp.arange(band, dtype=jnp.int32)
    live_slash = my_slash >= 1
    slash_hit = jnp.any(
        (my_slash[:, None, :] == offsets[None, :, None]) & live_slash[:, None, :], axis=2
    )
    band_ok = (
        slash_hit[:, None, :]
        & (offsets[None, None, :] >= 1)
        & ((block_ids[:, None] - offsets[None, :]) >= 0)[None, :, :]
    )
    causal = jnp.tril(jnp.ones((TILE_TOKENS, TILE_TOKENS), dtype=bool))
    own_tile = (offsets == 0)[None, None, None, :, None] & causal[None, None, :, None, :]
    band_allowed = band_ok[:, :, None, :, None] | own_tile
    repeats = jnp.any(
        ((block_ids[None, :, None] - my_vertical[:, None, :])[:, :, :, None] == my_slash[:, None, None, :])
        & live_slash[:, None, None, :],
        axis=3,
    )
    vert_ok = (
        (my_vertical[:, None, :] >= 0)
        & (my_vertical[:, None, :] < block_ids[None, :, None])
        & jnp.logical_not(repeats)
    )

    band_scores = (
        jnp.einsum(
            "bqhd,bkd->hbqk", q_b, band_k, preferred_element_type=jnp.float32
        ).reshape(per_dev, block_count, TILE_TOKENS, band, TILE_TOKENS)
        * score_scale
    )
    vert_scores = (
        jnp.einsum(
            "bqhd,hvkd->hbqvk", q_b, vert_k, preferred_element_type=jnp.float32
        )
        * score_scale
    )
    vert_allowed = vert_ok[:, :, None, :, None]
    neg = -jnp.inf
    row_top = jnp.maximum(
        jnp.max(jnp.where(band_allowed, band_scores, neg), axis=(3, 4)),
        jnp.max(jnp.where(vert_allowed, vert_scores, neg), axis=(3, 4)),
    )
    band_w = jnp.where(band_allowed, jnp.exp(band_scores - row_top[..., None, None]), 0.0)
    vert_w = jnp.where(vert_allowed, jnp.exp(vert_scores - row_top[..., None, None]), 0.0)
    row_total = jnp.sum(band_w, axis=(3, 4)) + jnp.sum(vert_w, axis=(3, 4))
    blended = jnp.einsum(
        "hbqk,bkd->hbqd",
        band_w.astype(jnp.bfloat16).reshape(per_dev, block_count, TILE_TOKENS, band * TILE_TOKENS),
        band_v,
        preferred_element_type=jnp.float32,
    ) + jnp.einsum(
        "hbqvk,hvkd->hbqd",
        vert_w.astype(jnp.bfloat16),
        vert_v,
        preferred_element_type=jnp.float32,
    )
    attended = (blended / row_total[..., None]).astype(jnp.bfloat16)
    attn_rows = attended.transpose(1, 2, 0, 3).reshape(ctx_rows, per_dev * HEAD_SIZE)
    token_attn = lax.all_to_all(attn_rows, "head", split_axis=0, concat_axis=1, tiled=True)

    weight_cols = lax.all_gather(out_weight, "cx", axis=1, tiled=True)
    attn_group = lax.all_gather(token_attn, "cz", axis=0, tiled=True)
    projected = jnp.dot(attn_group, weight_cols, preferred_element_type=jnp.float32).astype(
        jnp.bfloat16
    )
    return lax.all_to_all(projected, "cz", split_axis=0, concat_axis=1, tiled=True)


def solution(mesh):
    ctx_count = mesh.shape["ctx"]
    cx_count = 4 if ctx_count % 4 == 0 else 1
    split_mesh = Mesh(
        mesh.devices.reshape(ctx_count // cx_count, cx_count, mesh.shape["head"]),
        ("cz", "cx", "head"),
    )
    rows = P(("cz", "cx", "head"), None)
    placed = (rows, rows, rows, P(None, ("cz", "cx")), P(), P())
    return jax.shard_map(
        shards, mesh=split_mesh, in_specs=placed, out_specs=rows, check_vma=False
    )
```

```python
import numpy as np
import jax
import jax.numpy as jnp
from jax import lax
from jax.sharding import Mesh, PartitionSpec as P

HEAD_SIZE = 128
TILE_TOKENS = 128
CTX_AXES = ("cz", "cx")


def passed_along(block, axes, distance):
    count = 1
    for axis in axes:
        count *= lax.axis_size(axis)
    route = [(i - distance, i) for i in range(count) if i - distance >= 0]
    return lax.ppermute(block, axes, route)


def shards(queries, keys, values, out_weight, vertical, slash):
    head_count = lax.axis_size("head")
    head_index = lax.axis_index("head")
    cx_count = lax.axis_size("cx")
    ctx_index = lax.axis_index("cz") * cx_count + lax.axis_index("cx")
    tok_rows = queries.shape[0]
    query_heads = vertical.shape[0]
    kv_count = keys.shape[1] // HEAD_SIZE
    group_width = query_heads // kv_count
    per_dev = query_heads // head_count
    ctx_rows = tok_rows * head_count
    block_count = ctx_rows // TILE_TOKENS
    slash_span = block_count
    band = slash_span + 1

    kv_of_dest = (np.arange(head_count) * per_dev) // group_width
    q_part = queries.reshape(tok_rows, head_count, per_dev * HEAD_SIZE)
    k_part = jnp.take(keys.reshape(tok_rows, kv_count, HEAD_SIZE), kv_of_dest, axis=1)
    v_part = jnp.take(values.reshape(tok_rows, kv_count, HEAD_SIZE), kv_of_dest, axis=1)
    send = jnp.concatenate([q_part, k_part, v_part], axis=2).reshape(tok_rows, -1)
    recv = lax.all_to_all(send, "head", split_axis=1, concat_axis=0, tiled=True)
    q_width = per_dev * HEAD_SIZE
    q_loc = recv[:, :q_width]
    kv_loc = recv[:, q_width:]
    kv_prev = passed_along(kv_loc, CTX_AXES, 1)
    weight_cols = lax.all_gather(out_weight, "cx", axis=1, tiled=True)
    wide = jnp.concatenate([kv_prev, kv_loc], axis=0)

    my_heads = head_index * per_dev + jnp.arange(per_dev, dtype=jnp.int32)
    my_vertical = jnp.take(vertical, my_heads, axis=0)
    my_slash = jnp.take(slash, my_heads, axis=0)
    first_block = ctx_index * block_count
    local_vertical = my_vertical - first_block
    inside = (my_vertical >= 0) & (local_vertical >= 0) & (local_vertical < block_count)
    vertical_index = jnp.clip(local_vertical, 0, block_count - 1)
    kv_blocks = kv_loc.reshape(block_count, TILE_TOKENS, 2 * HEAD_SIZE)
    found = jnp.take(kv_blocks, vertical_index, axis=0)
    found = jnp.where(inside[:, :, None, None], found, jnp.zeros((), found.dtype))
    vertical_kv = lax.psum(found, CTX_AXES)
    vert_k = vertical_kv[..., :HEAD_SIZE]
    vert_v = vertical_kv[..., HEAD_SIZE:]

    band_kv = jnp.stack(
        [
            lax.slice_in_dim(
                wide, (b + block_count - slash_span) * TILE_TOKENS,
                (b + block_count + 1) * TILE_TOKENS, axis=0,
            )
            for b in range(block_count)
        ]
    )
    band_k = band_kv[..., :HEAD_SIZE]
    band_v = band_kv[..., HEAD_SIZE:]
    q_b = q_loc.reshape(block_count, TILE_TOKENS, per_dev, HEAD_SIZE)
    score_scale = HEAD_SIZE ** (-0.5)

    block_ids = first_block + jnp.arange(block_count, dtype=jnp.int32)
    offsets = slash_span - jnp.arange(band, dtype=jnp.int32)
    live_slash = my_slash >= 1
    slash_hit = jnp.any(
        (my_slash[:, None, :] == offsets[None, :, None]) & live_slash[:, None, :], axis=2
    )
    band_ok = (
        slash_hit[:, None, :]
        & (offsets[None, None, :] >= 1)
        & ((block_ids[:, None] - offsets[None, :]) >= 0)[None, :, :]
    )
    causal = jnp.tril(jnp.ones((TILE_TOKENS, TILE_TOKENS), dtype=bool))
    own_tile = (offsets == 0)[None, None, None, :, None] & causal[None, None, :, None, :]
    band_allowed = band_ok[:, :, None, :, None] | own_tile
    repeats = jnp.any(
        ((block_ids[None, :, None] - my_vertical[:, None, :])[:, :, :, None] == my_slash[:, None, None, :])
        & live_slash[:, None, None, :],
        axis=3,
    )
    vert_ok = (
        (my_vertical[:, None, :] >= 0)
        & (my_vertical[:, None, :] < block_ids[None, :, None])
        & jnp.logical_not(repeats)
    )

    band_scores = (
        jnp.einsum(
            "bqhd,bkd->hbqk", q_b, band_k, preferred_element_type=jnp.float32
        ).reshape(per_dev, block_count, TILE_TOKENS, band, TILE_TOKENS)
        * score_scale
    )
    vert_scores = (
        jnp.einsum(
            "bqhd,hvkd->hbqvk", q_b, vert_k, preferred_element_type=jnp.float32
        )
        * score_scale
    )
    vert_allowed = vert_ok[:, :, None, :, None]
    neg = -jnp.inf
    row_top = jnp.maximum(
        jnp.max(jnp.where(band_allowed, band_scores, neg), axis=(3, 4)),
        jnp.max(jnp.where(vert_allowed, vert_scores, neg), axis=(3, 4)),
    )
    band_w = jnp.where(band_allowed, jnp.exp(band_scores - row_top[..., None, None]), 0.0)
    vert_w = jnp.where(vert_allowed, jnp.exp(vert_scores - row_top[..., None, None]), 0.0)
    row_total = jnp.sum(band_w, axis=(3, 4)) + jnp.sum(vert_w, axis=(3, 4))
    blended = jnp.einsum(
        "hbqk,bkd->hbqd",
        band_w.astype(jnp.bfloat16).reshape(per_dev, block_count, TILE_TOKENS, band * TILE_TOKENS),
        band_v,
        preferred_element_type=jnp.float32,
    ) + jnp.einsum(
        "hbqvk,hvkd->hbqd",
        vert_w.astype(jnp.bfloat16),
        vert_v,
        preferred_element_type=jnp.float32,
    )
    attended = (blended / row_total[..., None]).astype(jnp.bfloat16)
    attended, weight_cols = lax.optimization_barrier((attended, weight_cols))
    attn_rows = attended.transpose(1, 2, 0, 3).reshape(ctx_rows, per_dev * HEAD_SIZE)
    token_attn = lax.all_to_all(attn_rows, "head", split_axis=0, concat_axis=1, tiled=True)

    attn_group = lax.all_gather(token_attn, "cz", axis=0, tiled=True)
    projected = jnp.dot(attn_group, weight_cols, preferred_element_type=jnp.float32).astype(
        jnp.bfloat16
    )
    return lax.all_to_all(projected, "cz", split_axis=0, concat_axis=1, tiled=True)


def solution(mesh):
    ctx_count = mesh.shape["ctx"]
    cx_count = 4 if ctx_count % 4 == 0 else 1
    split_mesh = Mesh(
        mesh.devices.reshape(ctx_count // cx_count, cx_count, mesh.shape["head"]),
        ("cz", "cx", "head"),
    )
    rows = P(("cz", "cx", "head"), None)
    placed = (rows, rows, rows, P(None, ("cz", "cx")), P(), P())
    return jax.shard_map(
        shards, mesh=split_mesh, in_specs=placed, out_specs=rows, check_vma=False
    )
```

```python
import numpy as np
import jax
import jax.numpy as jnp
from jax import lax
from jax.sharding import Mesh, PartitionSpec as P

HEAD_SIZE = 128
TILE_TOKENS = 128
CTX_AXES = ("cz", "cx")


def passed_along(block, axes, distance):
    count = 1
    for axis in axes:
        count *= lax.axis_size(axis)
    route = [(i - distance, i) for i in range(count) if i - distance >= 0]
    return lax.ppermute(block, axes, route)


def shards(queries, keys, values, out_weight, vertical, slash):
    head_count = lax.axis_size("head")
    head_index = lax.axis_index("head")
    cx_count = lax.axis_size("cx")
    ctx_index = lax.axis_index("cz") * cx_count + lax.axis_index("cx")
    tok_rows = queries.shape[0]
    query_heads = vertical.shape[0]
    kv_count = keys.shape[1] // HEAD_SIZE
    group_width = query_heads // kv_count
    per_dev = query_heads // head_count
    ctx_rows = tok_rows * head_count
    block_count = ctx_rows // TILE_TOKENS
    slash_span = block_count
    band = slash_span + 1

    kv_of_dest = (np.arange(head_count) * per_dev) // group_width
    q_part = queries.reshape(tok_rows, head_count, per_dev * HEAD_SIZE)
    k_part = jnp.take(keys.reshape(tok_rows, kv_count, HEAD_SIZE), kv_of_dest, axis=1)
    v_part = jnp.take(values.reshape(tok_rows, kv_count, HEAD_SIZE), kv_of_dest, axis=1)
    send = jnp.concatenate([q_part, k_part, v_part], axis=2).reshape(tok_rows, -1)
    recv = lax.all_to_all(send, "head", split_axis=1, concat_axis=0, tiled=True)
    q_width = per_dev * HEAD_SIZE
    q_loc = recv[:, :q_width]
    kv_loc = recv[:, q_width:]
    kv_prev = passed_along(kv_loc, CTX_AXES, 1)
    weight_cols = lax.all_gather(out_weight, "cx", axis=1, tiled=True)
    wide = jnp.concatenate([kv_prev, kv_loc], axis=0)

    my_heads = head_index * per_dev + jnp.arange(per_dev, dtype=jnp.int32)
    my_vertical = jnp.take(vertical, my_heads, axis=0)
    my_slash = jnp.take(slash, my_heads, axis=0)
    first_block = ctx_index * block_count
    local_vertical = my_vertical - first_block
    inside = (my_vertical >= 0) & (local_vertical >= 0) & (local_vertical < block_count)
    vertical_index = jnp.clip(local_vertical, 0, block_count - 1)
    kv_blocks = kv_loc.reshape(block_count, TILE_TOKENS, 2 * HEAD_SIZE)
    found = jnp.take(kv_blocks, vertical_index, axis=0)
    found = jnp.where(inside[:, :, None, None], found, jnp.zeros((), found.dtype))
    ctx_count = lax.axis_size("cz") * cx_count
    slot_shape = found.shape
    chunks = found.reshape(ctx_count, -1, TILE_TOKENS, 2 * HEAD_SIZE)
    gathered = lax.all_to_all(chunks, CTX_AXES, split_axis=0, concat_axis=0, tiled=True)
    reduced = jnp.sum(gathered.astype(jnp.float32), axis=0).astype(found.dtype)
    spread = jnp.broadcast_to(reduced[None], chunks.shape)
    vertical_kv = lax.all_to_all(spread, CTX_AXES, split_axis=0, concat_axis=0, tiled=True)
    vertical_kv = vertical_kv.reshape(slot_shape)
    vert_k = vertical_kv[..., :HEAD_SIZE]
    vert_v = vertical_kv[..., HEAD_SIZE:]

    band_kv = jnp.stack(
        [
            lax.slice_in_dim(
                wide, (b + block_count - slash_span) * TILE_TOKENS,
                (b + block_count + 1) * TILE_TOKENS, axis=0,
            )
            for b in range(block_count)
        ]
    )
    band_k = band_kv[..., :HEAD_SIZE]
    band_v = band_kv[..., HEAD_SIZE:]
    q_b = q_loc.reshape(block_count, TILE_TOKENS, per_dev, HEAD_SIZE)
    score_scale = HEAD_SIZE ** (-0.5)

    block_ids = first_block + jnp.arange(block_count, dtype=jnp.int32)
    offsets = slash_span - jnp.arange(band, dtype=jnp.int32)
    live_slash = my_slash >= 1
    slash_hit = jnp.any(
        (my_slash[:, None, :] == offsets[None, :, None]) & live_slash[:, None, :], axis=2
    )
    band_ok = (
        slash_hit[:, None, :]
        & (offsets[None, None, :] >= 1)
        & ((block_ids[:, None] - offsets[None, :]) >= 0)[None, :, :]
    )
    causal = jnp.tril(jnp.ones((TILE_TOKENS, TILE_TOKENS), dtype=bool))
    own_tile = (offsets == 0)[None, None, None, :, None] & causal[None, None, :, None, :]
    band_allowed = band_ok[:, :, None, :, None] | own_tile
    repeats = jnp.any(
        ((block_ids[None, :, None] - my_vertical[:, None, :])[:, :, :, None] == my_slash[:, None, None, :])
        & live_slash[:, None, None, :],
        axis=3,
    )
    vert_ok = (
        (my_vertical[:, None, :] >= 0)
        & (my_vertical[:, None, :] < block_ids[None, :, None])
        & jnp.logical_not(repeats)
    )

    band_scores = (
        jnp.einsum(
            "bqhd,bkd->hbqk", q_b, band_k, preferred_element_type=jnp.float32
        ).reshape(per_dev, block_count, TILE_TOKENS, band, TILE_TOKENS)
        * score_scale
    )
    vert_scores = (
        jnp.einsum(
            "bqhd,hvkd->hbqvk", q_b, vert_k, preferred_element_type=jnp.float32
        )
        * score_scale
    )
    vert_allowed = vert_ok[:, :, None, :, None]
    neg = -jnp.inf
    row_top = jnp.maximum(
        jnp.max(jnp.where(band_allowed, band_scores, neg), axis=(3, 4)),
        jnp.max(jnp.where(vert_allowed, vert_scores, neg), axis=(3, 4)),
    )
    band_w = jnp.where(band_allowed, jnp.exp(band_scores - row_top[..., None, None]), 0.0)
    vert_w = jnp.where(vert_allowed, jnp.exp(vert_scores - row_top[..., None, None]), 0.0)
    row_total = jnp.sum(band_w, axis=(3, 4)) + jnp.sum(vert_w, axis=(3, 4))
    blended = jnp.einsum(
        "hbqk,bkd->hbqd",
        band_w.astype(jnp.bfloat16).reshape(per_dev, block_count, TILE_TOKENS, band * TILE_TOKENS),
        band_v,
        preferred_element_type=jnp.float32,
    ) + jnp.einsum(
        "hbqvk,hvkd->hbqd",
        vert_w.astype(jnp.bfloat16),
        vert_v,
        preferred_element_type=jnp.float32,
    )
    attended = (blended / row_total[..., None]).astype(jnp.bfloat16)
    attended, weight_cols = lax.optimization_barrier((attended, weight_cols))
    attn_rows = attended.transpose(1, 2, 0, 3).reshape(ctx_rows, per_dev * HEAD_SIZE)
    token_attn = lax.all_to_all(attn_rows, "head", split_axis=0, concat_axis=1, tiled=True)

    attn_group = lax.all_gather(token_attn, "cz", axis=0, tiled=True)
    projected = jnp.dot(attn_group, weight_cols, preferred_element_type=jnp.float32).astype(
        jnp.bfloat16
    )
    return lax.all_to_all(projected, "cz", split_axis=0, concat_axis=1, tiled=True)


def solution(mesh):
    ctx_count = mesh.shape["ctx"]
    cx_count = 4 if ctx_count % 4 == 0 else 1
    split_mesh = Mesh(
        mesh.devices.reshape(ctx_count // cx_count, cx_count, mesh.shape["head"]),
        ("cz", "cx", "head"),
    )
    rows = P(("cz", "cx", "head"), None)
    placed = (rows, rows, rows, P(None, ("cz", "cx")), P(), P())
    return jax.shard_map(
        shards, mesh=split_mesh, in_specs=placed, out_specs=rows, check_vma=False
    )
```

```python
import numpy as np
import jax
import jax.numpy as jnp
from jax import lax
from jax.sharding import Mesh, PartitionSpec as P

HEAD_SIZE = 128
TILE_TOKENS = 128
CTX_AXES = ("cz", "cx")


def passed_along(block, axes, distance):
    count = 1
    for axis in axes:
        count *= lax.axis_size(axis)
    route = [(i - distance, i) for i in range(count) if i - distance >= 0]
    return lax.ppermute(block, axes, route)


def shards(queries, keys, values, out_weight, vertical, slash):
    head_count = lax.axis_size("head")
    head_index = lax.axis_index("head")
    cx_count = lax.axis_size("cx")
    ctx_index = lax.axis_index("cz") * cx_count + lax.axis_index("cx")
    tok_rows = queries.shape[0]
    query_heads = vertical.shape[0]
    kv_count = keys.shape[1] // HEAD_SIZE
    group_width = query_heads // kv_count
    per_dev = query_heads // head_count
    ctx_rows = tok_rows * head_count
    block_count = ctx_rows // TILE_TOKENS
    slash_span = block_count
    band = slash_span + 1

    kv_of_dest = (np.arange(head_count) * per_dev) // group_width
    q_part = queries.reshape(tok_rows, head_count, per_dev * HEAD_SIZE)
    k_part = jnp.take(keys.reshape(tok_rows, kv_count, HEAD_SIZE), kv_of_dest, axis=1)
    v_part = jnp.take(values.reshape(tok_rows, kv_count, HEAD_SIZE), kv_of_dest, axis=1)
    send = jnp.concatenate([q_part, k_part, v_part], axis=2).reshape(tok_rows, -1)
    recv = lax.all_to_all(send, "head", split_axis=1, concat_axis=0, tiled=True)
    q_width = per_dev * HEAD_SIZE
    q_loc = recv[:, :q_width]
    kv_loc = recv[:, q_width:]
    kv_prev = passed_along(kv_loc, CTX_AXES, 1)
    wide = jnp.concatenate([kv_prev, kv_loc], axis=0)

    my_heads = head_index * per_dev + jnp.arange(per_dev, dtype=jnp.int32)
    my_vertical = jnp.take(vertical, my_heads, axis=0)
    my_slash = jnp.take(slash, my_heads, axis=0)
    first_block = ctx_index * block_count
    local_vertical = my_vertical - first_block
    inside = (my_vertical >= 0) & (local_vertical >= 0) & (local_vertical < block_count)
    vertical_index = jnp.clip(local_vertical, 0, block_count - 1)
    kv_blocks = kv_loc.reshape(block_count, TILE_TOKENS, 2 * HEAD_SIZE)
    found = jnp.take(kv_blocks, vertical_index, axis=0)
    found = jnp.where(inside[:, :, None, None], found, jnp.zeros((), found.dtype))
    ctx_count = lax.axis_size("cz") * cx_count
    slot_shape = found.shape
    chunks = found.reshape(ctx_count, -1, TILE_TOKENS, 2 * HEAD_SIZE)
    gathered = lax.all_to_all(chunks, CTX_AXES, split_axis=0, concat_axis=0, tiled=True)
    reduced = jnp.sum(gathered.astype(jnp.float32), axis=0).astype(found.dtype)
    spread = jnp.broadcast_to(reduced[None], chunks.shape)
    vertical_kv = lax.all_to_all(spread, CTX_AXES, split_axis=0, concat_axis=0, tiled=True)
    vertical_kv = vertical_kv.reshape(slot_shape)
    vertical_kv, kv_prev_done, weight_part = lax.optimization_barrier((vertical_kv, wide, out_weight))
    wide = kv_prev_done
    weight_cols = lax.all_gather(weight_part, "cx", axis=1, tiled=True)
    vert_k = vertical_kv[..., :HEAD_SIZE]
    vert_v = vertical_kv[..., HEAD_SIZE:]

    band_kv = jnp.stack(
        [
            lax.slice_in_dim(
                wide, (b + block_count - slash_span) * TILE_TOKENS,
                (b + block_count + 1) * TILE_TOKENS, axis=0,
            )
            for b in range(block_count)
        ]
    )
    band_k = band_kv[..., :HEAD_SIZE]
    band_v = band_kv[..., HEAD_SIZE:]
    q_b = q_loc.reshape(block_count, TILE_TOKENS, per_dev, HEAD_SIZE)
    score_scale = HEAD_SIZE ** (-0.5)

    block_ids = first_block + jnp.arange(block_count, dtype=jnp.int32)
    offsets = slash_span - jnp.arange(band, dtype=jnp.int32)
    live_slash = my_slash >= 1
    slash_hit = jnp.any(
        (my_slash[:, None, :] == offsets[None, :, None]) & live_slash[:, None, :], axis=2
    )
    band_ok = (
        slash_hit[:, None, :]
        & (offsets[None, None, :] >= 1)
        & ((block_ids[:, None] - offsets[None, :]) >= 0)[None, :, :]
    )
    causal = jnp.tril(jnp.ones((TILE_TOKENS, TILE_TOKENS), dtype=bool))
    own_tile = (offsets == 0)[None, None, None, :, None] & causal[None, None, :, None, :]
    band_allowed = band_ok[:, :, None, :, None] | own_tile
    repeats = jnp.any(
        ((block_ids[None, :, None] - my_vertical[:, None, :])[:, :, :, None] == my_slash[:, None, None, :])
        & live_slash[:, None, None, :],
        axis=3,
    )
    vert_ok = (
        (my_vertical[:, None, :] >= 0)
        & (my_vertical[:, None, :] < block_ids[None, :, None])
        & jnp.logical_not(repeats)
    )

    band_scores = (
        jnp.einsum(
            "bqhd,bkd->hbqk", q_b, band_k, preferred_element_type=jnp.float32
        ).reshape(per_dev, block_count, TILE_TOKENS, band, TILE_TOKENS)
        * score_scale
    )
    vert_scores = (
        jnp.einsum(
            "bqhd,hvkd->hbqvk", q_b, vert_k, preferred_element_type=jnp.float32
        )
        * score_scale
    )
    vert_allowed = vert_ok[:, :, None, :, None]
    neg = -jnp.inf
    row_top = jnp.maximum(
        jnp.max(jnp.where(band_allowed, band_scores, neg), axis=(3, 4)),
        jnp.max(jnp.where(vert_allowed, vert_scores, neg), axis=(3, 4)),
    )
    band_w = jnp.where(band_allowed, jnp.exp(band_scores - row_top[..., None, None]), 0.0)
    vert_w = jnp.where(vert_allowed, jnp.exp(vert_scores - row_top[..., None, None]), 0.0)
    row_total = jnp.sum(band_w, axis=(3, 4)) + jnp.sum(vert_w, axis=(3, 4))
    blended = jnp.einsum(
        "hbqk,bkd->hbqd",
        band_w.astype(jnp.bfloat16).reshape(per_dev, block_count, TILE_TOKENS, band * TILE_TOKENS),
        band_v,
        preferred_element_type=jnp.float32,
    ) + jnp.einsum(
        "hbqvk,hvkd->hbqd",
        vert_w.astype(jnp.bfloat16),
        vert_v,
        preferred_element_type=jnp.float32,
    )
    attended = (blended / row_total[..., None]).astype(jnp.bfloat16)
    attended, weight_cols = lax.optimization_barrier((attended, weight_cols))
    attn_rows = attended.transpose(1, 2, 0, 3).reshape(ctx_rows, per_dev * HEAD_SIZE)
    token_attn = lax.all_to_all(attn_rows, "head", split_axis=0, concat_axis=1, tiled=True)

    attn_group = lax.all_gather(token_attn, "cz", axis=0, tiled=True)
    projected = jnp.dot(attn_group, weight_cols, preferred_element_type=jnp.float32).astype(
        jnp.bfloat16
    )
    return lax.all_to_all(projected, "cz", split_axis=0, concat_axis=1, tiled=True)


def solution(mesh):
    ctx_count = mesh.shape["ctx"]
    cx_count = 4 if ctx_count % 4 == 0 else 1
    split_mesh = Mesh(
        mesh.devices.reshape(ctx_count // cx_count, cx_count, mesh.shape["head"]),
        ("cz", "cx", "head"),
    )
    rows = P(("cz", "cx", "head"), None)
    placed = (rows, rows, rows, P(None, ("cz", "cx")), P(), P())
    return jax.shard_map(
        shards, mesh=split_mesh, in_specs=placed, out_specs=rows, check_vma=False
    )
```

```python
import numpy as np
import jax
import jax.numpy as jnp
from jax import lax
from jax.sharding import Mesh, PartitionSpec as P

HEAD_SIZE = 128
TILE_TOKENS = 128
CTX_AXES = ("cz", "cx")


def passed_along(block, axes, distance):
    count = 1
    for axis in axes:
        count *= lax.axis_size(axis)
    route = [(i - distance, i) for i in range(count) if i - distance >= 0]
    return lax.ppermute(block, axes, route)


def shards(queries, keys, values, out_weight, vertical, slash):
    head_count = lax.axis_size("head")
    head_index = lax.axis_index("head")
    cx_count = lax.axis_size("cx")
    ctx_index = lax.axis_index("cz") * cx_count + lax.axis_index("cx")
    tok_rows = queries.shape[0]
    query_heads = vertical.shape[0]
    kv_count = keys.shape[1] // HEAD_SIZE
    group_width = query_heads // kv_count
    per_dev = query_heads // head_count
    ctx_rows = tok_rows * head_count
    block_count = ctx_rows // TILE_TOKENS
    slash_span = block_count
    band = slash_span + 1

    kv_of_dest = (np.arange(head_count) * per_dev) // group_width
    q_part = queries.reshape(tok_rows, head_count, per_dev * HEAD_SIZE)
    k_part = jnp.take(keys.reshape(tok_rows, kv_count, HEAD_SIZE), kv_of_dest, axis=1)
    v_part = jnp.take(values.reshape(tok_rows, kv_count, HEAD_SIZE), kv_of_dest, axis=1)
    send = jnp.concatenate([q_part, k_part, v_part], axis=2).reshape(tok_rows, -1)
    recv = lax.all_to_all(send, "head", split_axis=1, concat_axis=0, tiled=True)
    q_width = per_dev * HEAD_SIZE
    q_loc = recv[:, :q_width]
    kv_loc = recv[:, q_width:]
    kv_prev = passed_along(kv_loc, CTX_AXES, 1)
    weight_cols = lax.all_gather(out_weight, "cx", axis=1, tiled=True)
    wide = jnp.concatenate([kv_prev, kv_loc], axis=0)

    my_heads = head_index * per_dev + jnp.arange(per_dev, dtype=jnp.int32)
    my_vertical = jnp.take(vertical, my_heads, axis=0)
    my_slash = jnp.take(slash, my_heads, axis=0)
    first_block = ctx_index * block_count
    local_vertical = my_vertical - first_block
    inside = (my_vertical >= 0) & (local_vertical >= 0) & (local_vertical < block_count)
    vertical_index = jnp.clip(local_vertical, 0, block_count - 1)
    kv_blocks = kv_loc.reshape(block_count, TILE_TOKENS, 2 * HEAD_SIZE)
    found = jnp.take(kv_blocks, vertical_index, axis=0)
    found = jnp.where(inside[:, :, None, None], found, jnp.zeros((), found.dtype))
    ctx_count = lax.axis_size("cz") * cx_count
    slot_shape = found.shape
    chunks = found.reshape(ctx_count, -1, TILE_TOKENS, 2 * HEAD_SIZE)
    gathered = lax.all_to_all(chunks, CTX_AXES, split_axis=0, concat_axis=0, tiled=True)
    reduced = jnp.sum(gathered.astype(jnp.float32), axis=0).astype(found.dtype)
    spread = jnp.broadcast_to(reduced[None], chunks.shape)
    vertical_kv = lax.all_to_all(spread, CTX_AXES, split_axis=0, concat_axis=0, tiled=True)
    vertical_kv = vertical_kv.reshape(slot_shape)
    vert_k = vertical_kv[..., :HEAD_SIZE]
    vert_v = vertical_kv[..., HEAD_SIZE:]

    band_kv = jnp.stack(
        [
            lax.slice_in_dim(
                wide, (b + block_count - slash_span) * TILE_TOKENS,
                (b + block_count + 1) * TILE_TOKENS, axis=0,
            )
            for b in range(block_count)
        ]
    )
    band_k = band_kv[..., :HEAD_SIZE]
    band_v = band_kv[..., HEAD_SIZE:]
    q_b = q_loc.reshape(block_count, TILE_TOKENS, per_dev, HEAD_SIZE)
    score_scale = HEAD_SIZE ** (-0.5)

    block_ids = first_block + jnp.arange(block_count, dtype=jnp.int32)
    offsets = slash_span - jnp.arange(band, dtype=jnp.int32)
    live_slash = my_slash >= 1
    slash_hit = jnp.any(
        (my_slash[:, None, :] == offsets[None, :, None]) & live_slash[:, None, :], axis=2
    )
    band_ok = (
        slash_hit[:, None, :]
        & (offsets[None, None, :] >= 1)
        & ((block_ids[:, None] - offsets[None, :]) >= 0)[None, :, :]
    )
    causal = jnp.tril(jnp.ones((TILE_TOKENS, TILE_TOKENS), dtype=bool))
    own_tile = (offsets == 0)[None, None, None, :, None] & causal[None, None, :, None, :]
    band_allowed = band_ok[:, :, None, :, None] | own_tile
    repeats = jnp.any(
        ((block_ids[None, :, None] - my_vertical[:, None, :])[:, :, :, None] == my_slash[:, None, None, :])
        & live_slash[:, None, None, :],
        axis=3,
    )
    vert_ok = (
        (my_vertical[:, None, :] >= 0)
        & (my_vertical[:, None, :] < block_ids[None, :, None])
        & jnp.logical_not(repeats)
    )

    band_scores = (
        jnp.einsum(
            "bqhd,bkd->hbqk", q_b, band_k, preferred_element_type=jnp.float32
        ).reshape(per_dev, block_count, TILE_TOKENS, band, TILE_TOKENS)
        * score_scale
    )
    vert_scores = (
        jnp.einsum(
            "bqhd,hvkd->hbqvk", q_b, vert_k, preferred_element_type=jnp.float32
        )
        * score_scale
    )
    vert_allowed = vert_ok[:, :, None, :, None]
    neg = -jnp.inf
    row_top = jnp.maximum(
        jnp.max(jnp.where(band_allowed, band_scores, neg), axis=(3, 4)),
        jnp.max(jnp.where(vert_allowed, vert_scores, neg), axis=(3, 4)),
    )
    band_w = jnp.where(band_allowed, jnp.exp(band_scores - row_top[..., None, None]), 0.0)
    vert_w = jnp.where(vert_allowed, jnp.exp(vert_scores - row_top[..., None, None]), 0.0)
    row_total = jnp.sum(band_w, axis=(3, 4)) + jnp.sum(vert_w, axis=(3, 4))
    blended = jnp.einsum(
        "hbqk,bkd->hbqd",
        band_w.astype(jnp.bfloat16).reshape(per_dev, block_count, TILE_TOKENS, band * TILE_TOKENS),
        band_v,
        preferred_element_type=jnp.float32,
    ) + jnp.einsum(
        "hbqvk,hvkd->hbqd",
        vert_w.astype(jnp.bfloat16),
        vert_v,
        preferred_element_type=jnp.float32,
    )
    attended = (blended / row_total[..., None]).astype(jnp.bfloat16)
    attended, weight_cols = lax.optimization_barrier((attended, weight_cols))
    cz_count = lax.axis_size("cz")
    tiles = attended.transpose(1, 2, 0, 3).reshape(block_count, TILE_TOKENS, per_dev * HEAD_SIZE)
    spread_tiles = jnp.broadcast_to(tiles[None], (cz_count,) + tiles.shape).reshape(
        cz_count * block_count, TILE_TOKENS, per_dev * HEAD_SIZE
    )
    got = lax.all_to_all(spread_tiles, ("cz", "head"), split_axis=0, concat_axis=0, tiled=True)
    attn_group = (
        got.reshape(cz_count, head_count, TILE_TOKENS, per_dev * HEAD_SIZE)
        .transpose(0, 2, 1, 3)
        .reshape(cz_count * TILE_TOKENS, query_heads * HEAD_SIZE)
    )
    projected = jnp.dot(attn_group, weight_cols, preferred_element_type=jnp.float32).astype(
        jnp.bfloat16
    )
    return lax.all_to_all(projected, "cz", split_axis=0, concat_axis=1, tiled=True)


def solution(mesh):
    ctx_count = mesh.shape["ctx"]
    cx_count = 4 if ctx_count % 4 == 0 else 1
    split_mesh = Mesh(
        mesh.devices.reshape(ctx_count // cx_count, cx_count, mesh.shape["head"]),
        ("cz", "cx", "head"),
    )
    rows = P(("cz", "cx", "head"), None)
    placed = (rows, rows, rows, P(None, ("cz", "cx")), P(), P())
    return jax.shard_map(
        shards, mesh=split_mesh, in_specs=placed, out_specs=rows, check_vma=False
    )
```

```python
import numpy as np
import jax
import jax.numpy as jnp
from jax import lax
from jax.sharding import Mesh, PartitionSpec as P

HEAD_SIZE = 128
TILE_TOKENS = 128
CTX_AXES = ("cz", "cx")


def passed_along(block, axes, distance):
    count = 1
    for axis in axes:
        count *= lax.axis_size(axis)
    route = [(i - distance, i) for i in range(count) if i - distance >= 0]
    return lax.ppermute(block, axes, route)


def shards(queries, keys, values, out_weight, vertical, slash):
    head_count = lax.axis_size("head")
    head_index = lax.axis_index("head")
    cx_count = lax.axis_size("cx")
    ctx_index = lax.axis_index("cz") * cx_count + lax.axis_index("cx")
    tok_rows = queries.shape[0]
    query_heads = vertical.shape[0]
    kv_count = keys.shape[1] // HEAD_SIZE
    group_width = query_heads // kv_count
    per_dev = query_heads // head_count
    ctx_rows = tok_rows * head_count
    block_count = ctx_rows // TILE_TOKENS
    slash_span = block_count
    band = slash_span + 1

    kv_of_dest = (np.arange(head_count) * per_dev) // group_width
    q_part = queries.reshape(tok_rows, head_count, per_dev * HEAD_SIZE)
    k_part = jnp.take(keys.reshape(tok_rows, kv_count, HEAD_SIZE), kv_of_dest, axis=1)
    v_part = jnp.take(values.reshape(tok_rows, kv_count, HEAD_SIZE), kv_of_dest, axis=1)
    send = jnp.concatenate([q_part, k_part, v_part], axis=2).reshape(tok_rows, -1)
    recv = lax.all_to_all(send, "head", split_axis=1, concat_axis=0, tiled=True)
    q_width = per_dev * HEAD_SIZE
    q_loc = recv[:, :q_width]
    kv_loc = recv[:, q_width:]
    kv_prev = passed_along(kv_loc, CTX_AXES, 1)
    weight_cols = lax.all_gather(out_weight, "cx", axis=1, tiled=True)
    wide = jnp.concatenate([kv_prev, kv_loc], axis=0)

    my_heads = head_index * per_dev + jnp.arange(per_dev, dtype=jnp.int32)
    my_vertical = jnp.take(vertical, my_heads, axis=0)
    my_slash = jnp.take(slash, my_heads, axis=0)
    first_block = ctx_index * block_count
    local_vertical = my_vertical - first_block
    inside = (my_vertical >= 0) & (local_vertical >= 0) & (local_vertical < block_count)
    vertical_index = jnp.clip(local_vertical, 0, block_count - 1)
    kv_blocks = kv_loc.reshape(block_count, TILE_TOKENS, 2 * HEAD_SIZE)
    found = jnp.take(kv_blocks, vertical_index, axis=0)
    found = jnp.where(inside[:, :, None, None], found, jnp.zeros((), found.dtype))
    ctx_count = lax.axis_size("cz") * cx_count
    slot_shape = found.shape
    chunks = found.reshape(ctx_count, -1, TILE_TOKENS, 2 * HEAD_SIZE)
    gathered = lax.all_to_all(chunks, CTX_AXES, split_axis=0, concat_axis=0, tiled=True)
    reduced = jnp.sum(gathered.astype(jnp.float32), axis=0).astype(found.dtype)
    spread = jnp.broadcast_to(reduced[None], chunks.shape)
    vertical_kv = lax.all_to_all(spread, CTX_AXES, split_axis=0, concat_axis=0, tiled=True)
    vertical_kv = vertical_kv.reshape(slot_shape)
    vert_k = vertical_kv[..., :HEAD_SIZE]
    vert_v = vertical_kv[..., HEAD_SIZE:]

    band_kv = jnp.stack(
        [
            lax.slice_in_dim(
                wide, (b + block_count - slash_span) * TILE_TOKENS,
                (b + block_count + 1) * TILE_TOKENS, axis=0,
            )
            for b in range(block_count)
        ]
    )
    band_k = band_kv[..., :HEAD_SIZE]
    band_v = band_kv[..., HEAD_SIZE:]
    q_b = q_loc.reshape(block_count, TILE_TOKENS, per_dev, HEAD_SIZE)
    score_scale = HEAD_SIZE ** (-0.5)

    block_ids = first_block + jnp.arange(block_count, dtype=jnp.int32)
    offsets = slash_span - jnp.arange(band, dtype=jnp.int32)
    live_slash = my_slash >= 1
    slash_hit = jnp.any(
        (my_slash[:, None, :] == offsets[None, :, None]) & live_slash[:, None, :], axis=2
    )
    band_ok = (
        slash_hit[:, None, :]
        & (offsets[None, None, :] >= 1)
        & ((block_ids[:, None] - offsets[None, :]) >= 0)[None, :, :]
    )
    causal = jnp.tril(jnp.ones((TILE_TOKENS, TILE_TOKENS), dtype=bool))
    own_tile = (offsets == 0)[None, None, None, :, None] & causal[None, None, :, None, :]
    band_allowed = band_ok[:, :, None, :, None] | own_tile
    repeats = jnp.any(
        ((block_ids[None, :, None] - my_vertical[:, None, :])[:, :, :, None] == my_slash[:, None, None, :])
        & live_slash[:, None, None, :],
        axis=3,
    )
    vert_ok = (
        (my_vertical[:, None, :] >= 0)
        & (my_vertical[:, None, :] < block_ids[None, :, None])
        & jnp.logical_not(repeats)
    )

    band_scores = (
        jnp.einsum(
            "bqhd,bkd->hbqk", q_b, band_k, preferred_element_type=jnp.float32
        ).reshape(per_dev, block_count, TILE_TOKENS, band, TILE_TOKENS)
        * score_scale
    )
    vert_allowed = vert_ok[:, :, None, :, None]
    neg = -jnp.inf
    band_top = jnp.max(jnp.where(band_allowed, band_scores, neg), axis=(3, 4))
    band_w = jnp.where(band_allowed, jnp.exp(band_scores - band_top[..., None, None]), 0.0)
    band_total = jnp.sum(band_w, axis=(3, 4))
    band_out = jnp.einsum(
        "hbqk,bkd->hbqd",
        band_w.astype(jnp.bfloat16).reshape(per_dev, block_count, TILE_TOKENS, band * TILE_TOKENS),
        band_v,
        preferred_element_type=jnp.float32,
    )
    band_out, band_total, band_top, vertical_kv = lax.optimization_barrier(
        (band_out, band_total, band_top, vertical_kv)
    )
    vert_k = vertical_kv[..., :HEAD_SIZE]
    vert_v = vertical_kv[..., HEAD_SIZE:]
    vert_scores = (
        jnp.einsum(
            "bqhd,hvkd->hbqvk", q_b, vert_k, preferred_element_type=jnp.float32
        )
        * score_scale
    )
    row_top = jnp.maximum(band_top, jnp.max(jnp.where(vert_allowed, vert_scores, neg), axis=(3, 4)))
    vert_w = jnp.where(vert_allowed, jnp.exp(vert_scores - row_top[..., None, None]), 0.0)
    band_scale = jnp.exp(band_top - row_top)
    row_total = band_total * band_scale + jnp.sum(vert_w, axis=(3, 4))
    blended = band_out * band_scale[..., None] + jnp.einsum(
        "hbqvk,hvkd->hbqd",
        vert_w.astype(jnp.bfloat16),
        vert_v,
        preferred_element_type=jnp.float32,
    )
    attended = (blended / row_total[..., None]).astype(jnp.bfloat16)
    attended, weight_cols = lax.optimization_barrier((attended, weight_cols))
    cz_count = lax.axis_size("cz")
    tiles = attended.transpose(1, 2, 0, 3).reshape(block_count, TILE_TOKENS, per_dev * HEAD_SIZE)
    spread_tiles = jnp.broadcast_to(tiles[None], (cz_count,) + tiles.shape).reshape(
        cz_count * block_count, TILE_TOKENS, per_dev * HEAD_SIZE
    )
    got = lax.all_to_all(spread_tiles, ("cz", "head"), split_axis=0, concat_axis=0, tiled=True)
    attn_group = (
        got.reshape(cz_count, head_count, TILE_TOKENS, per_dev * HEAD_SIZE)
        .transpose(0, 2, 1, 3)
        .reshape(cz_count * TILE_TOKENS, query_heads * HEAD_SIZE)
    )
    projected = jnp.dot(attn_group, weight_cols, preferred_element_type=jnp.float32).astype(
        jnp.bfloat16
    )
    return lax.all_to_all(projected, "cz", split_axis=0, concat_axis=1, tiled=True)


def solution(mesh):
    ctx_count = mesh.shape["ctx"]
    cx_count = 4 if ctx_count % 4 == 0 else 1
    split_mesh = Mesh(
        mesh.devices.reshape(ctx_count // cx_count, cx_count, mesh.shape["head"]),
        ("cz", "cx", "head"),
    )
    rows = P(("cz", "cx", "head"), None)
    placed = (rows, rows, rows, P(None, ("cz", "cx")), P(), P())
    return jax.shard_map(
        shards, mesh=split_mesh, in_specs=placed, out_specs=rows, check_vma=False
    )
```

```python
import numpy as np
import jax
import jax.numpy as jnp
from jax import lax
from jax.sharding import Mesh, PartitionSpec as P

HEAD_SIZE = 128
TILE_TOKENS = 128
CTX_AXES = ("cz", "cx")
HEAD_AXES = ("hy", "hc")


def passed_along(block, axes, distance):
    count = 1
    for axis in axes:
        count *= lax.axis_size(axis)
    route = [(i - distance, i) for i in range(count) if i - distance >= 0]
    return lax.ppermute(block, axes, route)


def shards(queries, keys, values, out_weight, vertical, slash):
    head_count = lax.axis_size("hy") * lax.axis_size("hc")
    head_index = lax.axis_index("hy") * lax.axis_size("hc") + lax.axis_index("hc")
    cx_count = lax.axis_size("cx")
    ctx_index = lax.axis_index("cz") * cx_count + lax.axis_index("cx")
    tok_rows = queries.shape[0]
    query_heads = vertical.shape[0]
    kv_count = keys.shape[1] // HEAD_SIZE
    group_width = query_heads // kv_count
    per_dev = query_heads // head_count
    ctx_rows = tok_rows * head_count
    block_count = ctx_rows // TILE_TOKENS
    slash_span = block_count
    band = slash_span + 1

    kv_of_dest = (np.arange(head_count) * per_dev) // group_width
    q_part = queries.reshape(tok_rows, head_count, per_dev * HEAD_SIZE)
    k_part = jnp.take(keys.reshape(tok_rows, kv_count, HEAD_SIZE), kv_of_dest, axis=1)
    v_part = jnp.take(values.reshape(tok_rows, kv_count, HEAD_SIZE), kv_of_dest, axis=1)
    send = jnp.concatenate([q_part, k_part, v_part], axis=2).reshape(tok_rows, -1)
    recv = lax.all_to_all(send, HEAD_AXES, split_axis=1, concat_axis=0, tiled=True)
    q_width = per_dev * HEAD_SIZE
    q_loc = recv[:, :q_width]
    kv_loc = recv[:, q_width:]
    kv_prev = passed_along(kv_loc, CTX_AXES, 1)
    core_count = lax.axis_size("hc")
    half_rows = out_weight.shape[0] // core_count
    weight_half = lax.dynamic_slice_in_dim(out_weight, lax.axis_index("hc") * half_rows, half_rows, axis=0)
    weight_half = lax.all_gather(weight_half, "cx", axis=1, tiled=True)
    weight_cols = lax.all_gather(weight_half, "hc", axis=0, tiled=True)
    wide = jnp.concatenate([kv_prev, kv_loc], axis=0)

    my_heads = head_index * per_dev + jnp.arange(per_dev, dtype=jnp.int32)
    my_vertical = jnp.take(vertical, my_heads, axis=0)
    my_slash = jnp.take(slash, my_heads, axis=0)
    first_block = ctx_index * block_count
    local_vertical = my_vertical - first_block
    inside = (my_vertical >= 0) & (local_vertical >= 0) & (local_vertical < block_count)
    vertical_index = jnp.clip(local_vertical, 0, block_count - 1)
    kv_blocks = kv_loc.reshape(block_count, TILE_TOKENS, 2 * HEAD_SIZE)
    found = jnp.take(kv_blocks, vertical_index, axis=0)
    found = jnp.where(inside[:, :, None, None], found, jnp.zeros((), found.dtype))
    ctx_count = lax.axis_size("cz") * cx_count
    slot_shape = found.shape
    chunks = found.reshape(ctx_count, -1, TILE_TOKENS, 2 * HEAD_SIZE)
    gathered = lax.all_to_all(chunks, CTX_AXES, split_axis=0, concat_axis=0, tiled=True)
    reduced = jnp.sum(gathered.astype(jnp.float32), axis=0).astype(found.dtype)
    spread = jnp.broadcast_to(reduced[None], chunks.shape)
    vertical_kv = lax.all_to_all(spread, CTX_AXES, split_axis=0, concat_axis=0, tiled=True)
    vertical_kv = vertical_kv.reshape(slot_shape)
    vert_k = vertical_kv[..., :HEAD_SIZE]
    vert_v = vertical_kv[..., HEAD_SIZE:]

    band_kv = jnp.stack(
        [
            lax.slice_in_dim(
                wide, (b + block_count - slash_span) * TILE_TOKENS,
                (b + block_count + 1) * TILE_TOKENS, axis=0,
            )
            for b in range(block_count)
        ]
    )
    band_k = band_kv[..., :HEAD_SIZE]
    band_v = band_kv[..., HEAD_SIZE:]
    q_b = q_loc.reshape(block_count, TILE_TOKENS, per_dev, HEAD_SIZE)
    score_scale = HEAD_SIZE ** (-0.5)

    block_ids = first_block + jnp.arange(block_count, dtype=jnp.int32)
    offsets = slash_span - jnp.arange(band, dtype=jnp.int32)
    live_slash = my_slash >= 1
    slash_hit = jnp.any(
        (my_slash[:, None, :] == offsets[None, :, None]) & live_slash[:, None, :], axis=2
    )
    band_ok = (
        slash_hit[:, None, :]
        & (offsets[None, None, :] >= 1)
        & ((block_ids[:, None] - offsets[None, :]) >= 0)[None, :, :]
    )
    causal = jnp.tril(jnp.ones((TILE_TOKENS, TILE_TOKENS), dtype=bool))
    own_tile = (offsets == 0)[None, None, None, :, None] & causal[None, None, :, None, :]
    band_allowed = band_ok[:, :, None, :, None] | own_tile
    repeats = jnp.any(
        ((block_ids[None, :, None] - my_vertical[:, None, :])[:, :, :, None] == my_slash[:, None, None, :])
        & live_slash[:, None, None, :],
        axis=3,
    )
    vert_ok = (
        (my_vertical[:, None, :] >= 0)
        & (my_vertical[:, None, :] < block_ids[None, :, None])
        & jnp.logical_not(repeats)
    )

    band_scores = (
        jnp.einsum(
            "bqhd,bkd->hbqk", q_b, band_k, preferred_element_type=jnp.float32
        ).reshape(per_dev, block_count, TILE_TOKENS, band, TILE_TOKENS)
        * score_scale
    )
    vert_allowed = vert_ok[:, :, None, :, None]
    neg = -jnp.inf
    band_top = jnp.max(jnp.where(band_allowed, band_scores, neg), axis=(3, 4))
    band_w = jnp.where(band_allowed, jnp.exp(band_scores - band_top[..., None, None]), 0.0)
    band_total = jnp.sum(band_w, axis=(3, 4))
    band_out = jnp.einsum(
        "hbqk,bkd->hbqd",
        band_w.astype(jnp.bfloat16).reshape(per_dev, block_count, TILE_TOKENS, band * TILE_TOKENS),
        band_v,
        preferred_element_type=jnp.float32,
    )
    band_out, band_total, band_top, vertical_kv = lax.optimization_barrier(
        (band_out, band_total, band_top, vertical_kv)
    )
    vert_k = vertical_kv[..., :HEAD_SIZE]
    vert_v = vertical_kv[..., HEAD_SIZE:]
    vert_scores = (
        jnp.einsum(
            "bqhd,hvkd->hbqvk", q_b, vert_k, preferred_element_type=jnp.float32
        )
        * score_scale
    )
    row_top = jnp.maximum(band_top, jnp.max(jnp.where(vert_allowed, vert_scores, neg), axis=(3, 4)))
    vert_w = jnp.where(vert_allowed, jnp.exp(vert_scores - row_top[..., None, None]), 0.0)
    band_scale = jnp.exp(band_top - row_top)
    row_total = band_total * band_scale + jnp.sum(vert_w, axis=(3, 4))
    blended = band_out * band_scale[..., None] + jnp.einsum(
        "hbqvk,hvkd->hbqd",
        vert_w.astype(jnp.bfloat16),
        vert_v,
        preferred_element_type=jnp.float32,
    )
    attended = (blended / row_total[..., None]).astype(jnp.bfloat16)
    attended, weight_cols = lax.optimization_barrier((attended, weight_cols))
    cz_count = lax.axis_size("cz")
    tiles = attended.transpose(1, 2, 0, 3).reshape(block_count, TILE_TOKENS, per_dev * HEAD_SIZE)
    spread_tiles = jnp.broadcast_to(tiles[None], (cz_count,) + tiles.shape).reshape(
        cz_count * block_count, TILE_TOKENS, per_dev * HEAD_SIZE
    )
    got = lax.all_to_all(spread_tiles, ("cz",) + HEAD_AXES, split_axis=0, concat_axis=0, tiled=True)
    attn_group = (
        got.reshape(cz_count, head_count, TILE_TOKENS, per_dev * HEAD_SIZE)
        .transpose(0, 2, 1, 3)
        .reshape(cz_count * TILE_TOKENS, query_heads * HEAD_SIZE)
    )
    projected = jnp.dot(attn_group, weight_cols, preferred_element_type=jnp.float32).astype(
        jnp.bfloat16
    )
    return lax.all_to_all(projected, "cz", split_axis=0, concat_axis=1, tiled=True)


def solution(mesh):
    ctx_count = mesh.shape["ctx"]
    cx_count = 4 if ctx_count % 4 == 0 else 1
    head_total = mesh.shape["head"]
    split_mesh = Mesh(
        mesh.devices.reshape(ctx_count // cx_count, cx_count, head_total // 2, 2),
        ("cz", "cx") + HEAD_AXES,
    )
    rows = P(("cz", "cx") + HEAD_AXES, None)
    placed = (rows, rows, rows, P(None, ("cz", "cx")), P(), P())
    return jax.shard_map(
        shards, mesh=split_mesh, in_specs=placed, out_specs=rows, check_vma=False
    )
```

```python
import numpy as np
import jax
import jax.numpy as jnp
from jax import lax
from jax.sharding import Mesh, PartitionSpec as P

HEAD_SIZE = 128
TILE_TOKENS = 128
CTX_AXES = ("cz", "cx")
HEAD_AXES = ("hy", "hc")


def passed_along(block, axes, distance):
    count = 1
    for axis in axes:
        count *= lax.axis_size(axis)
    route = [(i - distance, i) for i in range(count) if i - distance >= 0]
    return lax.ppermute(block, axes, route)


def shards(queries, keys, values, out_weight, vertical, slash):
    head_count = lax.axis_size("hy") * lax.axis_size("hc")
    head_index = lax.axis_index("hy") * lax.axis_size("hc") + lax.axis_index("hc")
    cx_count = lax.axis_size("cx")
    ctx_index = lax.axis_index("cz") * cx_count + lax.axis_index("cx")
    tok_rows = queries.shape[0]
    query_heads = vertical.shape[0]
    kv_count = keys.shape[1] // HEAD_SIZE
    group_width = query_heads // kv_count
    per_dev = query_heads // head_count
    ctx_rows = tok_rows * head_count
    block_count = ctx_rows // TILE_TOKENS
    slash_span = block_count
    band = slash_span + 1

    kv_of_dest = (np.arange(head_count) * per_dev) // group_width
    q_part = queries.reshape(tok_rows, head_count, per_dev * HEAD_SIZE)
    k_part = jnp.take(keys.reshape(tok_rows, kv_count, HEAD_SIZE), kv_of_dest, axis=1)
    v_part = jnp.take(values.reshape(tok_rows, kv_count, HEAD_SIZE), kv_of_dest, axis=1)
    send = jnp.concatenate([q_part, k_part, v_part], axis=2).reshape(tok_rows, -1)
    recv = lax.all_to_all(send, HEAD_AXES, split_axis=1, concat_axis=0, tiled=True)
    q_width = per_dev * HEAD_SIZE
    q_loc = recv[:, :q_width]
    kv_loc = recv[:, q_width:]
    kv_prev = passed_along(kv_loc, CTX_AXES, 1)
    core_count = lax.axis_size("hc")
    half_rows = out_weight.shape[0] // core_count
    weight_half = lax.dynamic_slice_in_dim(out_weight, lax.axis_index("hc") * half_rows, half_rows, axis=0)
    weight_half = lax.all_gather(weight_half, "cx", axis=1, tiled=True)
    wide = jnp.concatenate([kv_prev, kv_loc], axis=0)

    my_heads = head_index * per_dev + jnp.arange(per_dev, dtype=jnp.int32)
    my_vertical = jnp.take(vertical, my_heads, axis=0)
    my_slash = jnp.take(slash, my_heads, axis=0)
    first_block = ctx_index * block_count
    local_vertical = my_vertical - first_block
    inside = (my_vertical >= 0) & (local_vertical >= 0) & (local_vertical < block_count)
    vertical_index = jnp.clip(local_vertical, 0, block_count - 1)
    kv_blocks = kv_loc.reshape(block_count, TILE_TOKENS, 2 * HEAD_SIZE)
    found = jnp.take(kv_blocks, vertical_index, axis=0)
    found = jnp.where(inside[:, :, None, None], found, jnp.zeros((), found.dtype))
    ctx_count = lax.axis_size("cz") * cx_count
    slot_shape = found.shape
    chunks = found.reshape(ctx_count, -1, TILE_TOKENS, 2 * HEAD_SIZE)
    gathered = lax.all_to_all(chunks, CTX_AXES, split_axis=0, concat_axis=0, tiled=True)
    reduced = jnp.sum(gathered.astype(jnp.float32), axis=0).astype(found.dtype)
    spread = jnp.broadcast_to(reduced[None], chunks.shape)
    vertical_kv = lax.all_to_all(spread, CTX_AXES, split_axis=0, concat_axis=0, tiled=True)
    vertical_kv = vertical_kv.reshape(slot_shape)
    vert_k = vertical_kv[..., :HEAD_SIZE]
    vert_v = vertical_kv[..., HEAD_SIZE:]

    band_kv = jnp.stack(
        [
            lax.slice_in_dim(
                wide, (b + block_count - slash_span) * TILE_TOKENS,
                (b + block_count + 1) * TILE_TOKENS, axis=0,
            )
            for b in range(block_count)
        ]
    )
    band_k = band_kv[..., :HEAD_SIZE]
    band_v = band_kv[..., HEAD_SIZE:]
    q_b = q_loc.reshape(block_count, TILE_TOKENS, per_dev, HEAD_SIZE)
    score_scale = HEAD_SIZE ** (-0.5)

    block_ids = first_block + jnp.arange(block_count, dtype=jnp.int32)
    offsets = slash_span - jnp.arange(band, dtype=jnp.int32)
    live_slash = my_slash >= 1
    slash_hit = jnp.any(
        (my_slash[:, None, :] == offsets[None, :, None]) & live_slash[:, None, :], axis=2
    )
    band_ok = (
        slash_hit[:, None, :]
        & (offsets[None, None, :] >= 1)
        & ((block_ids[:, None] - offsets[None, :]) >= 0)[None, :, :]
    )
    causal = jnp.tril(jnp.ones((TILE_TOKENS, TILE_TOKENS), dtype=bool))
    own_tile = (offsets == 0)[None, None, None, :, None] & causal[None, None, :, None, :]
    band_allowed = band_ok[:, :, None, :, None] | own_tile
    repeats = jnp.any(
        ((block_ids[None, :, None] - my_vertical[:, None, :])[:, :, :, None] == my_slash[:, None, None, :])
        & live_slash[:, None, None, :],
        axis=3,
    )
    vert_ok = (
        (my_vertical[:, None, :] >= 0)
        & (my_vertical[:, None, :] < block_ids[None, :, None])
        & jnp.logical_not(repeats)
    )

    band_scores = (
        jnp.einsum(
            "bqhd,bkd->hbqk", q_b, band_k, preferred_element_type=jnp.float32
        ).reshape(per_dev, block_count, TILE_TOKENS, band, TILE_TOKENS)
        * score_scale
    )
    vert_allowed = vert_ok[:, :, None, :, None]
    neg = -jnp.inf
    band_top = jnp.max(jnp.where(band_allowed, band_scores, neg), axis=(3, 4))
    band_w = jnp.where(band_allowed, jnp.exp(band_scores - band_top[..., None, None]), 0.0)
    band_total = jnp.sum(band_w, axis=(3, 4))
    band_out = jnp.einsum(
        "hbqk,bkd->hbqd",
        band_w.astype(jnp.bfloat16).reshape(per_dev, block_count, TILE_TOKENS, band * TILE_TOKENS),
        band_v,
        preferred_element_type=jnp.float32,
    )
    band_out, band_total, band_top, vertical_kv, weight_half = lax.optimization_barrier(
        (band_out, band_total, band_top, vertical_kv, weight_half)
    )
    weight_cols = lax.all_gather(weight_half, "hc", axis=0, tiled=True)
    vert_k = vertical_kv[..., :HEAD_SIZE]
    vert_v = vertical_kv[..., HEAD_SIZE:]
    vert_scores = (
        jnp.einsum(
            "bqhd,hvkd->hbqvk", q_b, vert_k, preferred_element_type=jnp.float32
        )
        * score_scale
    )
    row_top = jnp.maximum(band_top, jnp.max(jnp.where(vert_allowed, vert_scores, neg), axis=(3, 4)))
    vert_w = jnp.where(vert_allowed, jnp.exp(vert_scores - row_top[..., None, None]), 0.0)
    band_scale = jnp.exp(band_top - row_top)
    row_total = band_total * band_scale + jnp.sum(vert_w, axis=(3, 4))
    blended = band_out * band_scale[..., None] + jnp.einsum(
        "hbqvk,hvkd->hbqd",
        vert_w.astype(jnp.bfloat16),
        vert_v,
        preferred_element_type=jnp.float32,
    )
    attended = (blended / row_total[..., None]).astype(jnp.bfloat16)
    cz_count = lax.axis_size("cz")
    tiles = attended.transpose(1, 2, 0, 3).reshape(block_count, TILE_TOKENS, per_dev * HEAD_SIZE)
    spread_tiles = jnp.broadcast_to(tiles[None], (cz_count,) + tiles.shape).reshape(
        cz_count * block_count, TILE_TOKENS, per_dev * HEAD_SIZE
    )
    got = lax.all_to_all(spread_tiles, ("cz",) + HEAD_AXES, split_axis=0, concat_axis=0, tiled=True)
    attn_group = (
        got.reshape(cz_count, head_count, TILE_TOKENS, per_dev * HEAD_SIZE)
        .transpose(0, 2, 1, 3)
        .reshape(cz_count * TILE_TOKENS, query_heads * HEAD_SIZE)
    )
    projected = jnp.dot(attn_group, weight_cols, preferred_element_type=jnp.float32).astype(
        jnp.bfloat16
    )
    return lax.all_to_all(projected, "cz", split_axis=0, concat_axis=1, tiled=True)


def solution(mesh):
    ctx_count = mesh.shape["ctx"]
    cx_count = 4 if ctx_count % 4 == 0 else 1
    head_total = mesh.shape["head"]
    split_mesh = Mesh(
        mesh.devices.reshape(ctx_count // cx_count, cx_count, head_total // 2, 2),
        ("cz", "cx") + HEAD_AXES,
    )
    rows = P(("cz", "cx") + HEAD_AXES, None)
    placed = (rows, rows, rows, P(None, ("cz", "cx")), P(), P())
    return jax.shard_map(
        shards, mesh=split_mesh, in_specs=placed, out_specs=rows, check_vma=False
    )
```

```python
import numpy as np
import jax
import jax.numpy as jnp
from jax import lax
from jax.sharding import Mesh, PartitionSpec as P

HEAD_SIZE = 128
TILE_TOKENS = 128
CTX_AXES = ("cz", "cx")
HEAD_AXES = ("hy", "hc")


def passed_along(block, axes, distance):
    count = 1
    for axis in axes:
        count *= lax.axis_size(axis)
    route = [(i - distance, i) for i in range(count) if i - distance >= 0]
    return lax.ppermute(block, axes, route)


def shards(queries, keys, values, out_weight, vertical, slash):
    head_count = lax.axis_size("hy") * lax.axis_size("hc")
    head_index = lax.axis_index("hy") * lax.axis_size("hc") + lax.axis_index("hc")
    cx_count = lax.axis_size("cx")
    ctx_index = lax.axis_index("cz") * cx_count + lax.axis_index("cx")
    tok_rows = queries.shape[0]
    query_heads = vertical.shape[0]
    kv_count = keys.shape[1] // HEAD_SIZE
    group_width = query_heads // kv_count
    per_dev = query_heads // head_count
    ctx_rows = tok_rows * head_count
    block_count = ctx_rows // TILE_TOKENS
    slash_span = block_count
    band = slash_span + 1

    kv_of_dest = (np.arange(head_count) * per_dev) // group_width
    q_part = queries.reshape(tok_rows, head_count, per_dev * HEAD_SIZE)
    k_part = jnp.take(keys.reshape(tok_rows, kv_count, HEAD_SIZE), kv_of_dest, axis=1)
    v_part = jnp.take(values.reshape(tok_rows, kv_count, HEAD_SIZE), kv_of_dest, axis=1)
    kv_send = jnp.concatenate([k_part, v_part], axis=2).reshape(tok_rows, -1)
    kv_loc = lax.all_to_all(kv_send, HEAD_AXES, split_axis=1, concat_axis=0, tiled=True)
    q_pieces = []
    for shift in range(head_count):
        if shift == 0:
            q_pieces.append(jnp.take(q_part, head_index, axis=1))
            continue
        outgoing = jnp.take(q_part, (head_index + shift) % head_count, axis=1)
        route = [(i, (i + shift) % head_count) for i in range(head_count)]
        q_pieces.append(lax.ppermute(outgoing, HEAD_AXES, route))
    source_order = (head_index - jnp.arange(head_count)) % head_count
    q_stack = jnp.stack(q_pieces)
    q_loc = jnp.take(q_stack, jnp.argsort(source_order), axis=0).reshape(ctx_rows, -1)
    kv_prev = passed_along(kv_loc, CTX_AXES, 1)
    core_count = lax.axis_size("hc")
    half_rows = out_weight.shape[0] // core_count
    weight_half = lax.dynamic_slice_in_dim(out_weight, lax.axis_index("hc") * half_rows, half_rows, axis=0)
    weight_half = lax.all_gather(weight_half, "cx", axis=1, tiled=True)
    weight_cols = lax.all_gather(weight_half, "hc", axis=0, tiled=True)
    wide = jnp.concatenate([kv_prev, kv_loc], axis=0)

    my_heads = head_index * per_dev + jnp.arange(per_dev, dtype=jnp.int32)
    my_vertical = jnp.take(vertical, my_heads, axis=0)
    my_slash = jnp.take(slash, my_heads, axis=0)
    first_block = ctx_index * block_count
    local_vertical = my_vertical - first_block
    inside = (my_vertical >= 0) & (local_vertical >= 0) & (local_vertical < block_count)
    vertical_index = jnp.clip(local_vertical, 0, block_count - 1)
    kv_blocks = kv_loc.reshape(block_count, TILE_TOKENS, 2 * HEAD_SIZE)
    found = jnp.take(kv_blocks, vertical_index, axis=0)
    found = jnp.where(inside[:, :, None, None], found, jnp.zeros((), found.dtype))
    ctx_count = lax.axis_size("cz") * cx_count
    slot_shape = found.shape
    chunks = found.reshape(ctx_count, -1, TILE_TOKENS, 2 * HEAD_SIZE)
    gathered = lax.all_to_all(chunks, CTX_AXES, split_axis=0, concat_axis=0, tiled=True)
    reduced = jnp.sum(gathered.astype(jnp.float32), axis=0).astype(found.dtype)
    spread = jnp.broadcast_to(reduced[None], chunks.shape)
    vertical_kv = lax.all_to_all(spread, CTX_AXES, split_axis=0, concat_axis=0, tiled=True)
    vertical_kv = vertical_kv.reshape(slot_shape)
    vert_k = vertical_kv[..., :HEAD_SIZE]
    vert_v = vertical_kv[..., HEAD_SIZE:]

    band_kv = jnp.stack(
        [
            lax.slice_in_dim(
                wide, (b + block_count - slash_span) * TILE_TOKENS,
                (b + block_count + 1) * TILE_TOKENS, axis=0,
            )
            for b in range(block_count)
        ]
    )
    band_k = band_kv[..., :HEAD_SIZE]
    band_v = band_kv[..., HEAD_SIZE:]
    q_b = q_loc.reshape(block_count, TILE_TOKENS, per_dev, HEAD_SIZE)
    score_scale = HEAD_SIZE ** (-0.5)

    block_ids = first_block + jnp.arange(block_count, dtype=jnp.int32)
    offsets = slash_span - jnp.arange(band, dtype=jnp.int32)
    live_slash = my_slash >= 1
    slash_hit = jnp.any(
        (my_slash[:, None, :] == offsets[None, :, None]) & live_slash[:, None, :], axis=2
    )
    band_ok = (
        slash_hit[:, None, :]
        & (offsets[None, None, :] >= 1)
        & ((block_ids[:, None] - offsets[None, :]) >= 0)[None, :, :]
    )
    causal = jnp.tril(jnp.ones((TILE_TOKENS, TILE_TOKENS), dtype=bool))
    own_tile = (offsets == 0)[None, None, None, :, None] & causal[None, None, :, None, :]
    band_allowed = band_ok[:, :, None, :, None] | own_tile
    repeats = jnp.any(
        ((block_ids[None, :, None] - my_vertical[:, None, :])[:, :, :, None] == my_slash[:, None, None, :])
        & live_slash[:, None, None, :],
        axis=3,
    )
    vert_ok = (
        (my_vertical[:, None, :] >= 0)
        & (my_vertical[:, None, :] < block_ids[None, :, None])
        & jnp.logical_not(repeats)
    )

    band_scores = (
        jnp.einsum(
            "bqhd,bkd->hbqk", q_b, band_k, preferred_element_type=jnp.float32
        ).reshape(per_dev, block_count, TILE_TOKENS, band, TILE_TOKENS)
        * score_scale
    )
    vert_allowed = vert_ok[:, :, None, :, None]
    neg = -jnp.inf
    band_top = jnp.max(jnp.where(band_allowed, band_scores, neg), axis=(3, 4))
    band_w = jnp.where(band_allowed, jnp.exp(band_scores - band_top[..., None, None]), 0.0)
    band_total = jnp.sum(band_w, axis=(3, 4))
    band_out = jnp.einsum(
        "hbqk,bkd->hbqd",
        band_w.astype(jnp.bfloat16).reshape(per_dev, block_count, TILE_TOKENS, band * TILE_TOKENS),
        band_v,
        preferred_element_type=jnp.float32,
    )
    band_out, band_total, band_top, vertical_kv = lax.optimization_barrier(
        (band_out, band_total, band_top, vertical_kv)
    )
    vert_k = vertical_kv[..., :HEAD_SIZE]
    vert_v = vertical_kv[..., HEAD_SIZE:]
    vert_scores = (
        jnp.einsum(
            "bqhd,hvkd->hbqvk", q_b, vert_k, preferred_element_type=jnp.float32
        )
        * score_scale
    )
    row_top = jnp.maximum(band_top, jnp.max(jnp.where(vert_allowed, vert_scores, neg), axis=(3, 4)))
    vert_w = jnp.where(vert_allowed, jnp.exp(vert_scores - row_top[..., None, None]), 0.0)
    band_scale = jnp.exp(band_top - row_top)
    row_total = band_total * band_scale + jnp.sum(vert_w, axis=(3, 4))
    blended = band_out * band_scale[..., None] + jnp.einsum(
        "hbqvk,hvkd->hbqd",
        vert_w.astype(jnp.bfloat16),
        vert_v,
        preferred_element_type=jnp.float32,
    )
    attended = (blended / row_total[..., None]).astype(jnp.bfloat16)
    attended, weight_cols = lax.optimization_barrier((attended, weight_cols))
    cz_count = lax.axis_size("cz")
    tiles = attended.transpose(1, 2, 0, 3).reshape(block_count, TILE_TOKENS, per_dev * HEAD_SIZE)
    spread_tiles = jnp.broadcast_to(tiles[None], (cz_count,) + tiles.shape).reshape(
        cz_count * block_count, TILE_TOKENS, per_dev * HEAD_SIZE
    )
    got = lax.all_to_all(spread_tiles, ("cz",) + HEAD_AXES, split_axis=0, concat_axis=0, tiled=True)
    attn_group = (
        got.reshape(cz_count, head_count, TILE_TOKENS, per_dev * HEAD_SIZE)
        .transpose(0, 2, 1, 3)
        .reshape(cz_count * TILE_TOKENS, query_heads * HEAD_SIZE)
    )
    projected = jnp.dot(attn_group, weight_cols, preferred_element_type=jnp.float32).astype(
        jnp.bfloat16
    )
    return lax.all_to_all(projected, "cz", split_axis=0, concat_axis=1, tiled=True)


def solution(mesh):
    ctx_count = mesh.shape["ctx"]
    cx_count = 4 if ctx_count % 4 == 0 else 1
    head_total = mesh.shape["head"]
    split_mesh = Mesh(
        mesh.devices.reshape(ctx_count // cx_count, cx_count, head_total // 2, 2),
        ("cz", "cx") + HEAD_AXES,
    )
    rows = P(("cz", "cx") + HEAD_AXES, None)
    placed = (rows, rows, rows, P(None, ("cz", "cx")), P(), P())
    return jax.shard_map(
        shards, mesh=split_mesh, in_specs=placed, out_specs=rows, check_vma=False
    )
```

```python
import numpy as np
import jax
import jax.numpy as jnp
from jax import lax
from jax.sharding import Mesh, PartitionSpec as P

HEAD_SIZE = 128
TILE_TOKENS = 128
CTX_AXES = ("cz", "cx")
HEAD_AXES = ("hy", "hc")


def passed_along(block, axes, distance):
    count = 1
    for axis in axes:
        count *= lax.axis_size(axis)
    route = [(i - distance, i) for i in range(count) if i - distance >= 0]
    return lax.ppermute(block, axes, route)


def shards(queries, keys, values, out_weight, vertical, slash):
    head_count = lax.axis_size("hy") * lax.axis_size("hc")
    head_index = lax.axis_index("hy") * lax.axis_size("hc") + lax.axis_index("hc")
    cx_count = lax.axis_size("cx")
    ctx_index = lax.axis_index("cz") * cx_count + lax.axis_index("cx")
    tok_rows = queries.shape[0]
    query_heads = vertical.shape[0]
    kv_count = keys.shape[1] // HEAD_SIZE
    group_width = query_heads // kv_count
    per_dev = query_heads // head_count
    ctx_rows = tok_rows * head_count
    block_count = ctx_rows // TILE_TOKENS
    slash_span = block_count
    band = slash_span + 1

    kv_of_dest = (np.arange(head_count) * per_dev) // group_width
    q_part = queries.reshape(tok_rows, head_count, per_dev * HEAD_SIZE)
    k_part = jnp.take(keys.reshape(tok_rows, kv_count, HEAD_SIZE), kv_of_dest, axis=1)
    v_part = jnp.take(values.reshape(tok_rows, kv_count, HEAD_SIZE), kv_of_dest, axis=1)
    send = jnp.concatenate([q_part, k_part, v_part], axis=2).reshape(tok_rows, -1)
    recv = lax.all_to_all(send, HEAD_AXES, split_axis=1, concat_axis=0, tiled=True)
    q_width = per_dev * HEAD_SIZE
    q_loc = recv[:, :q_width]
    kv_loc = recv[:, q_width:]
    kv_prev = passed_along(kv_loc, CTX_AXES, 1)
    core_count = lax.axis_size("hc")
    half_rows = out_weight.shape[0] // core_count
    weight_half = lax.dynamic_slice_in_dim(out_weight, lax.axis_index("hc") * half_rows, half_rows, axis=0)
    weight_half = lax.all_gather(weight_half, "cx", axis=1, tiled=True)
    weight_cols = lax.all_gather(weight_half, "hc", axis=0, tiled=True)
    wide = jnp.concatenate([kv_prev, kv_loc], axis=0)

    my_heads = head_index * per_dev + jnp.arange(per_dev, dtype=jnp.int32)
    my_vertical = jnp.take(vertical, my_heads, axis=0)
    my_slash = jnp.take(slash, my_heads, axis=0)
    first_block = ctx_index * block_count
    local_vertical = my_vertical - first_block
    inside = (my_vertical >= 0) & (local_vertical >= 0) & (local_vertical < block_count)
    vertical_index = jnp.clip(local_vertical, 0, block_count - 1)
    kv_blocks = kv_loc.reshape(block_count, TILE_TOKENS, 2 * HEAD_SIZE)
    found = jnp.take(kv_blocks, vertical_index, axis=0)
    found = jnp.where(inside[:, :, None, None], found, jnp.zeros((), found.dtype))
    ctx_count = lax.axis_size("cz") * cx_count
    slot_shape = found.shape
    chunks = found.reshape(ctx_count, -1, TILE_TOKENS, 2 * HEAD_SIZE)
    gathered = lax.all_to_all(chunks, CTX_AXES, split_axis=0, concat_axis=0, tiled=True)
    reduced = jnp.sum(gathered.astype(jnp.float32), axis=0).astype(found.dtype)
    spread = jnp.broadcast_to(reduced[None], chunks.shape)
    vertical_kv = lax.all_to_all(spread, CTX_AXES, split_axis=0, concat_axis=0, tiled=True)
    vertical_kv = vertical_kv.reshape(slot_shape)
    vert_k = vertical_kv[..., :HEAD_SIZE]
    vert_v = vertical_kv[..., HEAD_SIZE:]

    band_kv = jnp.stack(
        [
            lax.slice_in_dim(
                wide, (b + block_count - slash_span) * TILE_TOKENS,
                (b + block_count + 1) * TILE_TOKENS, axis=0,
            )
            for b in range(block_count)
        ]
    )
    band_k = band_kv[..., :HEAD_SIZE]
    band_v = band_kv[..., HEAD_SIZE:]
    q_b = q_loc.reshape(block_count, TILE_TOKENS, per_dev, HEAD_SIZE)
    score_scale = HEAD_SIZE ** (-0.5)

    block_ids = first_block + jnp.arange(block_count, dtype=jnp.int32)
    offsets = slash_span - jnp.arange(band, dtype=jnp.int32)
    live_slash = my_slash >= 1
    slash_hit = jnp.any(
        (my_slash[:, None, :] == offsets[None, :, None]) & live_slash[:, None, :], axis=2
    )
    band_ok = (
        slash_hit[:, None, :]
        & (offsets[None, None, :] >= 1)
        & ((block_ids[:, None] - offsets[None, :]) >= 0)[None, :, :]
    )
    causal = jnp.tril(jnp.ones((TILE_TOKENS, TILE_TOKENS), dtype=bool))
    own_tile = (offsets == 0)[None, None, None, :, None] & causal[None, None, :, None, :]
    band_allowed = band_ok[:, :, None, :, None] | own_tile
    repeats = jnp.any(
        ((block_ids[None, :, None] - my_vertical[:, None, :])[:, :, :, None] == my_slash[:, None, None, :])
        & live_slash[:, None, None, :],
        axis=3,
    )
    vert_ok = (
        (my_vertical[:, None, :] >= 0)
        & (my_vertical[:, None, :] < block_ids[None, :, None])
        & jnp.logical_not(repeats)
    )

    band_scores = (
        jnp.einsum(
            "bqhd,bkd->hbqk", q_b, band_k, preferred_element_type=jnp.float32
        ).reshape(per_dev, block_count, TILE_TOKENS, band, TILE_TOKENS)
        * score_scale
    )
    vert_allowed = vert_ok[:, :, None, :, None]
    neg = -jnp.inf
    band_top = jnp.max(jnp.where(band_allowed, band_scores, neg), axis=(3, 4))
    band_w = jnp.where(band_allowed, jnp.exp(band_scores - band_top[..., None, None]), 0.0)
    band_total = jnp.sum(band_w, axis=(3, 4))
    band_out = jnp.einsum(
        "hbqk,bkd->hbqd",
        band_w.astype(jnp.bfloat16).reshape(per_dev, block_count, TILE_TOKENS, band * TILE_TOKENS),
        band_v,
        preferred_element_type=jnp.float32,
    )
    band_out, band_total, band_top, vertical_kv = lax.optimization_barrier(
        (band_out, band_total, band_top, vertical_kv)
    )
    vert_k = vertical_kv[..., :HEAD_SIZE]
    vert_v = vertical_kv[..., HEAD_SIZE:]
    vert_scores = (
        jnp.einsum(
            "bqhd,hvkd->hbqvk", q_b, vert_k, preferred_element_type=jnp.float32
        )
        * score_scale
    )
    row_top = jnp.maximum(band_top, jnp.max(jnp.where(vert_allowed, vert_scores, neg), axis=(3, 4)))
    vert_w = jnp.where(vert_allowed, jnp.exp(vert_scores - row_top[..., None, None]), 0.0)
    band_scale = jnp.exp(band_top - row_top)
    row_total = band_total * band_scale + jnp.sum(vert_w, axis=(3, 4))
    blended = band_out * band_scale[..., None] + jnp.einsum(
        "hbqvk,hvkd->hbqd",
        vert_w.astype(jnp.bfloat16),
        vert_v,
        preferred_element_type=jnp.float32,
    )
    attended = (blended / row_total[..., None]).astype(jnp.bfloat16)
    attended, weight_cols = lax.optimization_barrier((attended, weight_cols))
    cz_count = lax.axis_size("cz")
    tiles = attended.transpose(1, 2, 0, 3).reshape(block_count, TILE_TOKENS, per_dev * HEAD_SIZE)
    spread_tiles = jnp.broadcast_to(tiles[None], (cz_count,) + tiles.shape).reshape(
        cz_count * block_count, TILE_TOKENS, per_dev * HEAD_SIZE
    )
    got = lax.all_to_all(spread_tiles, ("cz",) + HEAD_AXES, split_axis=0, concat_axis=0, tiled=True)
    attn_group = got.reshape(cz_count, head_count, TILE_TOKENS, per_dev * HEAD_SIZE)
    projected = jnp.einsum(
        "zhtd,hdn->ztn",
        attn_group,
        weight_cols.reshape(head_count, per_dev * HEAD_SIZE, -1),
        preferred_element_type=jnp.float32,
    ).astype(jnp.bfloat16).reshape(cz_count * TILE_TOKENS, -1)
    return lax.all_to_all(projected, "cz", split_axis=0, concat_axis=1, tiled=True)


def solution(mesh):
    ctx_count = mesh.shape["ctx"]
    cx_count = 4 if ctx_count % 4 == 0 else 1
    head_total = mesh.shape["head"]
    split_mesh = Mesh(
        mesh.devices.reshape(ctx_count // cx_count, cx_count, head_total // 2, 2),
        ("cz", "cx") + HEAD_AXES,
    )
    rows = P(("cz", "cx") + HEAD_AXES, None)
    placed = (rows, rows, rows, P(None, ("cz", "cx")), P(), P())
    return jax.shard_map(
        shards, mesh=split_mesh, in_specs=placed, out_specs=rows, check_vma=False
    )
```

```python
import numpy as np
import jax
import jax.numpy as jnp
from jax import lax
from jax.sharding import Mesh, PartitionSpec as P

HEAD_SIZE = 128
TILE_TOKENS = 128
CTX_AXES = ("cz", "cx")
HEAD_AXES = ("hy", "hc")


def passed_along(block, axes, distance):
    count = 1
    for axis in axes:
        count *= lax.axis_size(axis)
    route = [(i - distance, i) for i in range(count) if i - distance >= 0]
    return lax.ppermute(block, axes, route)


def shards(queries, keys, values, out_weight, vertical, slash):
    head_count = lax.axis_size("hy") * lax.axis_size("hc")
    head_index = lax.axis_index("hy") * lax.axis_size("hc") + lax.axis_index("hc")
    cx_count = lax.axis_size("cx")
    ctx_index = lax.axis_index("cz") * cx_count + lax.axis_index("cx")
    tok_rows = queries.shape[0]
    query_heads = vertical.shape[0]
    kv_count = keys.shape[1] // HEAD_SIZE
    group_width = query_heads // kv_count
    per_dev = query_heads // head_count
    ctx_rows = tok_rows * head_count
    block_count = ctx_rows // TILE_TOKENS
    slash_span = block_count
    band = slash_span + 1

    core_count = lax.axis_size("hc")
    hy_count = lax.axis_size("hy")
    group_of = (np.arange(head_count) % core_count) * hy_count + np.arange(head_count) // core_count
    kv_of_dest = (group_of * per_dev) // group_width
    q_part = jnp.take(queries.reshape(tok_rows, head_count, per_dev * HEAD_SIZE), group_of, axis=1)
    k_part = jnp.take(keys.reshape(tok_rows, kv_count, HEAD_SIZE), kv_of_dest, axis=1)
    v_part = jnp.take(values.reshape(tok_rows, kv_count, HEAD_SIZE), kv_of_dest, axis=1)
    send = jnp.concatenate([q_part, k_part, v_part], axis=2).reshape(tok_rows, -1)
    recv = lax.all_to_all(send, HEAD_AXES, split_axis=1, concat_axis=0, tiled=True)
    q_width = per_dev * HEAD_SIZE
    q_loc = recv[:, :q_width]
    kv_loc = recv[:, q_width:]
    kv_prev = passed_along(kv_loc, CTX_AXES, 1)
    half_rows = out_weight.shape[0] // core_count
    weight_half = lax.dynamic_slice_in_dim(out_weight, lax.axis_index("hc") * half_rows, half_rows, axis=0)
    weight_half = lax.all_gather(weight_half, "cx", axis=1, tiled=True)
    wide = jnp.concatenate([kv_prev, kv_loc], axis=0)

    my_heads = jnp.asarray(group_of, jnp.int32)[head_index] * per_dev + jnp.arange(per_dev, dtype=jnp.int32)
    my_vertical = jnp.take(vertical, my_heads, axis=0)
    my_slash = jnp.take(slash, my_heads, axis=0)
    first_block = ctx_index * block_count
    local_vertical = my_vertical - first_block
    inside = (my_vertical >= 0) & (local_vertical >= 0) & (local_vertical < block_count)
    vertical_index = jnp.clip(local_vertical, 0, block_count - 1)
    kv_blocks = kv_loc.reshape(block_count, TILE_TOKENS, 2 * HEAD_SIZE)
    found = jnp.take(kv_blocks, vertical_index, axis=0)
    found = jnp.where(inside[:, :, None, None], found, jnp.zeros((), found.dtype))
    ctx_count = lax.axis_size("cz") * cx_count
    slot_shape = found.shape
    chunks = found.reshape(ctx_count, -1, TILE_TOKENS, 2 * HEAD_SIZE)
    gathered = lax.all_to_all(chunks, CTX_AXES, split_axis=0, concat_axis=0, tiled=True)
    reduced = jnp.sum(gathered.astype(jnp.float32), axis=0).astype(found.dtype)
    spread = jnp.broadcast_to(reduced[None], chunks.shape)
    vertical_kv = lax.all_to_all(spread, CTX_AXES, split_axis=0, concat_axis=0, tiled=True)
    vertical_kv = vertical_kv.reshape(slot_shape)
    vert_k = vertical_kv[..., :HEAD_SIZE]
    vert_v = vertical_kv[..., HEAD_SIZE:]

    band_kv = jnp.stack(
        [
            lax.slice_in_dim(
                wide, (b + block_count - slash_span) * TILE_TOKENS,
                (b + block_count + 1) * TILE_TOKENS, axis=0,
            )
            for b in range(block_count)
        ]
    )
    band_k = band_kv[..., :HEAD_SIZE]
    band_v = band_kv[..., HEAD_SIZE:]
    q_b = q_loc.reshape(block_count, TILE_TOKENS, per_dev, HEAD_SIZE)
    score_scale = HEAD_SIZE ** (-0.5)

    block_ids = first_block + jnp.arange(block_count, dtype=jnp.int32)
    offsets = slash_span - jnp.arange(band, dtype=jnp.int32)
    live_slash = my_slash >= 1
    slash_hit = jnp.any(
        (my_slash[:, None, :] == offsets[None, :, None]) & live_slash[:, None, :], axis=2
    )
    band_ok = (
        slash_hit[:, None, :]
        & (offsets[None, None, :] >= 1)
        & ((block_ids[:, None] - offsets[None, :]) >= 0)[None, :, :]
    )
    causal = jnp.tril(jnp.ones((TILE_TOKENS, TILE_TOKENS), dtype=bool))
    own_tile = (offsets == 0)[None, None, None, :, None] & causal[None, None, :, None, :]
    band_allowed = band_ok[:, :, None, :, None] | own_tile
    repeats = jnp.any(
        ((block_ids[None, :, None] - my_vertical[:, None, :])[:, :, :, None] == my_slash[:, None, None, :])
        & live_slash[:, None, None, :],
        axis=3,
    )
    vert_ok = (
        (my_vertical[:, None, :] >= 0)
        & (my_vertical[:, None, :] < block_ids[None, :, None])
        & jnp.logical_not(repeats)
    )

    band_scores = (
        jnp.einsum(
            "bqhd,bkd->hbqk", q_b, band_k, preferred_element_type=jnp.float32
        ).reshape(per_dev, block_count, TILE_TOKENS, band, TILE_TOKENS)
        * score_scale
    )
    vert_allowed = vert_ok[:, :, None, :, None]
    neg = -jnp.inf
    band_top = jnp.max(jnp.where(band_allowed, band_scores, neg), axis=(3, 4))
    band_w = jnp.where(band_allowed, jnp.exp(band_scores - band_top[..., None, None]), 0.0)
    band_total = jnp.sum(band_w, axis=(3, 4))
    band_out = jnp.einsum(
        "hbqk,bkd->hbqd",
        band_w.astype(jnp.bfloat16).reshape(per_dev, block_count, TILE_TOKENS, band * TILE_TOKENS),
        band_v,
        preferred_element_type=jnp.float32,
    )
    band_out, band_total, band_top, vertical_kv = lax.optimization_barrier(
        (band_out, band_total, band_top, vertical_kv)
    )
    vert_k = vertical_kv[..., :HEAD_SIZE]
    vert_v = vertical_kv[..., HEAD_SIZE:]
    vert_scores = (
        jnp.einsum(
            "bqhd,hvkd->hbqvk", q_b, vert_k, preferred_element_type=jnp.float32
        )
        * score_scale
    )
    row_top = jnp.maximum(band_top, jnp.max(jnp.where(vert_allowed, vert_scores, neg), axis=(3, 4)))
    vert_w = jnp.where(vert_allowed, jnp.exp(vert_scores - row_top[..., None, None]), 0.0)
    band_scale = jnp.exp(band_top - row_top)
    row_total = band_total * band_scale + jnp.sum(vert_w, axis=(3, 4))
    blended = band_out * band_scale[..., None] + jnp.einsum(
        "hbqvk,hvkd->hbqd",
        vert_w.astype(jnp.bfloat16),
        vert_v,
        preferred_element_type=jnp.float32,
    )
    attended = (blended / row_total[..., None]).astype(jnp.bfloat16)
    attended, weight_half = lax.optimization_barrier((attended, weight_half))
    cz_count = lax.axis_size("cz")
    tiles = attended.transpose(1, 2, 0, 3).reshape(
        hy_count, core_count * TILE_TOKENS, per_dev * HEAD_SIZE
    )
    spread_tiles = jnp.broadcast_to(tiles[None], (cz_count,) + tiles.shape).reshape(
        cz_count * hy_count, core_count * TILE_TOKENS, per_dev * HEAD_SIZE
    )
    got = lax.all_to_all(spread_tiles, ("cz", "hy"), split_axis=0, concat_axis=0, tiled=True)
    got = got.reshape(cz_count, hy_count, core_count, TILE_TOKENS, per_dev * HEAD_SIZE)
    partial = jnp.einsum(
        "zstqd,sdn->tzqn",
        got,
        weight_half.reshape(hy_count, per_dev * HEAD_SIZE, -1),
        preferred_element_type=jnp.float32,
    )
    core_index = lax.axis_index("hc")
    mine = jnp.take(partial, core_index, axis=0)
    theirs = jnp.take(partial, (core_index + 1) % core_count, axis=0)
    route = [(i, (i + 1) % core_count) for i in range(core_count)]
    projected = (mine + lax.ppermute(theirs, "hc", route)).astype(jnp.bfloat16)
    projected = projected.reshape(cz_count * TILE_TOKENS, -1)
    return lax.all_to_all(projected, "cz", split_axis=0, concat_axis=1, tiled=True)


def solution(mesh):
    ctx_count = mesh.shape["ctx"]
    cx_count = 4 if ctx_count % 4 == 0 else 1
    head_total = mesh.shape["head"]
    split_mesh = Mesh(
        mesh.devices.reshape(ctx_count // cx_count, cx_count, head_total // 2, 2),
        ("cz", "cx") + HEAD_AXES,
    )
    rows = P(("cz", "cx") + HEAD_AXES, None)
    placed = (rows, rows, rows, P(None, ("cz", "cx")), P(), P())
    return jax.shard_map(
        shards, mesh=split_mesh, in_specs=placed, out_specs=rows, check_vma=False
    )
```

```python
import numpy as np
import jax
import jax.numpy as jnp
from jax import lax
from jax.sharding import Mesh, PartitionSpec as P

HEAD_SIZE = 128
TILE_TOKENS = 128
CTX_AXES = ("cz", "cx")
HEAD_AXES = ("hy", "hc")


def passed_along(block, axes, distance):
    count = 1
    for axis in axes:
        count *= lax.axis_size(axis)
    route = [(i - distance, i) for i in range(count) if i - distance >= 0]
    return lax.ppermute(block, axes, route)


def shards(queries, keys, values, out_weight, vertical, slash):
    head_count = lax.axis_size("hy") * lax.axis_size("hc")
    head_index = lax.axis_index("hy") * lax.axis_size("hc") + lax.axis_index("hc")
    cx_count = lax.axis_size("cx")
    ctx_index = lax.axis_index("cz") * cx_count + lax.axis_index("cx")
    tok_rows = queries.shape[0]
    query_heads = vertical.shape[0]
    kv_count = keys.shape[1] // HEAD_SIZE
    group_width = query_heads // kv_count
    per_dev = query_heads // head_count
    ctx_rows = tok_rows * head_count
    block_count = ctx_rows // TILE_TOKENS
    slash_span = block_count
    band = slash_span + 1

    kv_of_dest = (np.arange(head_count) * per_dev) // group_width
    q_part = queries.reshape(tok_rows, head_count, per_dev * HEAD_SIZE)
    k_part = jnp.take(keys.reshape(tok_rows, kv_count, HEAD_SIZE), kv_of_dest, axis=1)
    v_part = jnp.take(values.reshape(tok_rows, kv_count, HEAD_SIZE), kv_of_dest, axis=1)
    send = jnp.concatenate([q_part, k_part, v_part], axis=2).reshape(tok_rows, -1)
    recv = lax.all_to_all(send, HEAD_AXES, split_axis=1, concat_axis=0, tiled=True)
    q_width = per_dev * HEAD_SIZE
    q_loc = recv[:, :q_width]
    kv_loc = recv[:, q_width:]
    kv_prev = passed_along(kv_loc, CTX_AXES, 1)
    part_rows = out_weight.shape[0] // head_count
    weight_part = lax.dynamic_slice_in_dim(out_weight, head_index * part_rows, part_rows, axis=0)
    weight_part = lax.all_gather(weight_part, "cx", axis=1, tiled=True)
    weight_cols = lax.all_gather(weight_part, HEAD_AXES, axis=0, tiled=True)
    wide = jnp.concatenate([kv_prev, kv_loc], axis=0)

    my_heads = head_index * per_dev + jnp.arange(per_dev, dtype=jnp.int32)
    my_vertical = jnp.take(vertical, my_heads, axis=0)
    my_slash = jnp.take(slash, my_heads, axis=0)
    first_block = ctx_index * block_count
    local_vertical = my_vertical - first_block
    inside = (my_vertical >= 0) & (local_vertical >= 0) & (local_vertical < block_count)
    vertical_index = jnp.clip(local_vertical, 0, block_count - 1)
    kv_blocks = kv_loc.reshape(block_count, TILE_TOKENS, 2 * HEAD_SIZE)
    found = jnp.take(kv_blocks, vertical_index, axis=0)
    found = jnp.where(inside[:, :, None, None], found, jnp.zeros((), found.dtype))
    ctx_count = lax.axis_size("cz") * cx_count
    slot_shape = found.shape
    chunks = found.reshape(ctx_count, -1, TILE_TOKENS, 2 * HEAD_SIZE)
    gathered = lax.all_to_all(chunks, CTX_AXES, split_axis=0, concat_axis=0, tiled=True)
    reduced = jnp.sum(gathered.astype(jnp.float32), axis=0).astype(found.dtype)
    spread = jnp.broadcast_to(reduced[None], chunks.shape)
    vertical_kv = lax.all_to_all(spread, CTX_AXES, split_axis=0, concat_axis=0, tiled=True)
    vertical_kv = vertical_kv.reshape(slot_shape)
    vert_k = vertical_kv[..., :HEAD_SIZE]
    vert_v = vertical_kv[..., HEAD_SIZE:]

    band_kv = jnp.stack(
        [
            lax.slice_in_dim(
                wide, (b + block_count - slash_span) * TILE_TOKENS,
                (b + block_count + 1) * TILE_TOKENS, axis=0,
            )
            for b in range(block_count)
        ]
    )
    band_k = band_kv[..., :HEAD_SIZE]
    band_v = band_kv[..., HEAD_SIZE:]
    q_b = q_loc.reshape(block_count, TILE_TOKENS, per_dev, HEAD_SIZE)
    score_scale = HEAD_SIZE ** (-0.5)

    block_ids = first_block + jnp.arange(block_count, dtype=jnp.int32)
    offsets = slash_span - jnp.arange(band, dtype=jnp.int32)
    live_slash = my_slash >= 1
    slash_hit = jnp.any(
        (my_slash[:, None, :] == offsets[None, :, None]) & live_slash[:, None, :], axis=2
    )
    band_ok = (
        slash_hit[:, None, :]
        & (offsets[None, None, :] >= 1)
        & ((block_ids[:, None] - offsets[None, :]) >= 0)[None, :, :]
    )
    causal = jnp.tril(jnp.ones((TILE_TOKENS, TILE_TOKENS), dtype=bool))
    own_tile = (offsets == 0)[None, None, None, :, None] & causal[None, None, :, None, :]
    band_allowed = band_ok[:, :, None, :, None] | own_tile
    repeats = jnp.any(
        ((block_ids[None, :, None] - my_vertical[:, None, :])[:, :, :, None] == my_slash[:, None, None, :])
        & live_slash[:, None, None, :],
        axis=3,
    )
    vert_ok = (
        (my_vertical[:, None, :] >= 0)
        & (my_vertical[:, None, :] < block_ids[None, :, None])
        & jnp.logical_not(repeats)
    )

    band_scores = (
        jnp.einsum(
            "bqhd,bkd->hbqk", q_b, band_k, preferred_element_type=jnp.float32
        ).reshape(per_dev, block_count, TILE_TOKENS, band, TILE_TOKENS)
        * score_scale
    )
    vert_allowed = vert_ok[:, :, None, :, None]
    neg = -jnp.inf
    band_top = jnp.max(jnp.where(band_allowed, band_scores, neg), axis=(3, 4))
    band_w = jnp.where(band_allowed, jnp.exp(band_scores - band_top[..., None, None]), 0.0)
    band_total = jnp.sum(band_w, axis=(3, 4))
    band_out = jnp.einsum(
        "hbqk,bkd->hbqd",
        band_w.astype(jnp.bfloat16).reshape(per_dev, block_count, TILE_TOKENS, band * TILE_TOKENS),
        band_v,
        preferred_element_type=jnp.float32,
    )
    band_out, band_total, band_top, vertical_kv = lax.optimization_barrier(
        (band_out, band_total, band_top, vertical_kv)
    )
    vert_k = vertical_kv[..., :HEAD_SIZE]
    vert_v = vertical_kv[..., HEAD_SIZE:]
    vert_scores = (
        jnp.einsum(
            "bqhd,hvkd->hbqvk", q_b, vert_k, preferred_element_type=jnp.float32
        )
        * score_scale
    )
    row_top = jnp.maximum(band_top, jnp.max(jnp.where(vert_allowed, vert_scores, neg), axis=(3, 4)))
    vert_w = jnp.where(vert_allowed, jnp.exp(vert_scores - row_top[..., None, None]), 0.0)
    band_scale = jnp.exp(band_top - row_top)
    row_total = band_total * band_scale + jnp.sum(vert_w, axis=(3, 4))
    blended = band_out * band_scale[..., None] + jnp.einsum(
        "hbqvk,hvkd->hbqd",
        vert_w.astype(jnp.bfloat16),
        vert_v,
        preferred_element_type=jnp.float32,
    )
    attended = (blended / row_total[..., None]).astype(jnp.bfloat16)
    attended, weight_cols = lax.optimization_barrier((attended, weight_cols))
    cz_count = lax.axis_size("cz")
    tiles = attended.transpose(1, 2, 0, 3).reshape(block_count, TILE_TOKENS, per_dev * HEAD_SIZE)
    spread_tiles = jnp.broadcast_to(tiles[None], (cz_count,) + tiles.shape).reshape(
        cz_count * block_count, TILE_TOKENS, per_dev * HEAD_SIZE
    )
    got = lax.all_to_all(spread_tiles, ("cz",) + HEAD_AXES, split_axis=0, concat_axis=0, tiled=True)
    attn_group = got.reshape(cz_count, head_count, TILE_TOKENS, per_dev * HEAD_SIZE)
    projected = jnp.einsum(
        "zhtd,hdn->ztn",
        attn_group,
        weight_cols.reshape(head_count, per_dev * HEAD_SIZE, -1),
        preferred_element_type=jnp.float32,
    ).astype(jnp.bfloat16).reshape(cz_count * TILE_TOKENS, -1)
    return lax.all_to_all(projected, "cz", split_axis=0, concat_axis=1, tiled=True)


def solution(mesh):
    ctx_count = mesh.shape["ctx"]
    cx_count = 4 if ctx_count % 4 == 0 else 1
    head_total = mesh.shape["head"]
    split_mesh = Mesh(
        mesh.devices.reshape(ctx_count // cx_count, cx_count, head_total // 2, 2),
        ("cz", "cx") + HEAD_AXES,
    )
    rows = P(("cz", "cx") + HEAD_AXES, None)
    placed = (rows, rows, rows, P(None, ("cz", "cx")), P(), P())
    return jax.shard_map(
        shards, mesh=split_mesh, in_specs=placed, out_specs=rows, check_vma=False
    )
```

```python
import numpy as np
import jax
import jax.numpy as jnp
from jax import lax
from jax.sharding import Mesh, PartitionSpec as P

HEAD_SIZE = 128
TILE_TOKENS = 128
CTX_AXES = ("cz", "cx")
HEAD_AXES = ("hy", "hc")


def passed_along(block, axes, distance):
    count = 1
    for axis in axes:
        count *= lax.axis_size(axis)
    route = [(i - distance, i) for i in range(count) if i - distance >= 0]
    return lax.ppermute(block, axes, route)


def shards(queries, keys, values, out_weight, vertical, slash):
    head_count = lax.axis_size("hy") * lax.axis_size("hc")
    head_index = lax.axis_index("hy") * lax.axis_size("hc") + lax.axis_index("hc")
    cx_count = lax.axis_size("cx")
    ctx_index = lax.axis_index("cz") * cx_count + lax.axis_index("cx")
    tok_rows = queries.shape[0]
    query_heads = vertical.shape[0]
    kv_count = keys.shape[1] // HEAD_SIZE
    group_width = query_heads // kv_count
    per_dev = query_heads // head_count
    ctx_rows = tok_rows * head_count
    block_count = ctx_rows // TILE_TOKENS
    slash_span = block_count
    band = slash_span + 1

    kv_of_dest = (np.arange(head_count) * per_dev) // group_width
    q_part = queries.reshape(tok_rows, head_count, per_dev * HEAD_SIZE)
    k_part = jnp.take(keys.reshape(tok_rows, kv_count, HEAD_SIZE), kv_of_dest, axis=1)
    v_part = jnp.take(values.reshape(tok_rows, kv_count, HEAD_SIZE), kv_of_dest, axis=1)
    send = jnp.concatenate([q_part, k_part, v_part], axis=2).reshape(tok_rows, -1)
    recv = lax.all_to_all(send, HEAD_AXES, split_axis=1, concat_axis=0, tiled=True)
    q_width = per_dev * HEAD_SIZE
    q_loc = recv[:, :q_width]
    kv_loc = recv[:, q_width:]
    kv_prev = passed_along(kv_loc, CTX_AXES, 1)
    part_rows = out_weight.shape[0] // head_count
    weight_part = lax.dynamic_slice_in_dim(out_weight, head_index * part_rows, part_rows, axis=0)
    weight_part = lax.all_gather(weight_part, "cx", axis=1, tiled=True)
    kv_loc, weight_part = lax.optimization_barrier((kv_loc, weight_part))
    weight_cols = lax.all_gather(weight_part, HEAD_AXES, axis=0, tiled=True)
    wide = jnp.concatenate([kv_prev, kv_loc], axis=0)

    my_heads = head_index * per_dev + jnp.arange(per_dev, dtype=jnp.int32)
    my_vertical = jnp.take(vertical, my_heads, axis=0)
    my_slash = jnp.take(slash, my_heads, axis=0)
    first_block = ctx_index * block_count
    local_vertical = my_vertical - first_block
    inside = (my_vertical >= 0) & (local_vertical >= 0) & (local_vertical < block_count)
    vertical_index = jnp.clip(local_vertical, 0, block_count - 1)
    kv_blocks = kv_loc.reshape(block_count, TILE_TOKENS, 2 * HEAD_SIZE)
    found = jnp.take(kv_blocks, vertical_index, axis=0)
    found = jnp.where(inside[:, :, None, None], found, jnp.zeros((), found.dtype))
    ctx_count = lax.axis_size("cz") * cx_count
    slot_shape = found.shape
    chunks = found.reshape(ctx_count, -1, TILE_TOKENS, 2 * HEAD_SIZE)
    gathered = lax.all_to_all(chunks, CTX_AXES, split_axis=0, concat_axis=0, tiled=True)
    reduced = jnp.sum(gathered.astype(jnp.float32), axis=0).astype(found.dtype)
    spread = jnp.broadcast_to(reduced[None], chunks.shape)
    vertical_kv = lax.all_to_all(spread, CTX_AXES, split_axis=0, concat_axis=0, tiled=True)
    vertical_kv = vertical_kv.reshape(slot_shape)
    vert_k = vertical_kv[..., :HEAD_SIZE]
    vert_v = vertical_kv[..., HEAD_SIZE:]

    band_kv = jnp.stack(
        [
            lax.slice_in_dim(
                wide, (b + block_count - slash_span) * TILE_TOKENS,
                (b + block_count + 1) * TILE_TOKENS, axis=0,
            )
            for b in range(block_count)
        ]
    )
    band_k = band_kv[..., :HEAD_SIZE]
    band_v = band_kv[..., HEAD_SIZE:]
    q_b = q_loc.reshape(block_count, TILE_TOKENS, per_dev, HEAD_SIZE)
    score_scale = HEAD_SIZE ** (-0.5)

    block_ids = first_block + jnp.arange(block_count, dtype=jnp.int32)
    offsets = slash_span - jnp.arange(band, dtype=jnp.int32)
    live_slash = my_slash >= 1
    slash_hit = jnp.any(
        (my_slash[:, None, :] == offsets[None, :, None]) & live_slash[:, None, :], axis=2
    )
    band_ok = (
        slash_hit[:, None, :]
        & (offsets[None, None, :] >= 1)
        & ((block_ids[:, None] - offsets[None, :]) >= 0)[None, :, :]
    )
    causal = jnp.tril(jnp.ones((TILE_TOKENS, TILE_TOKENS), dtype=bool))
    own_tile = (offsets == 0)[None, None, None, :, None] & causal[None, None, :, None, :]
    band_allowed = band_ok[:, :, None, :, None] | own_tile
    repeats = jnp.any(
        ((block_ids[None, :, None] - my_vertical[:, None, :])[:, :, :, None] == my_slash[:, None, None, :])
        & live_slash[:, None, None, :],
        axis=3,
    )
    vert_ok = (
        (my_vertical[:, None, :] >= 0)
        & (my_vertical[:, None, :] < block_ids[None, :, None])
        & jnp.logical_not(repeats)
    )

    band_scores = (
        jnp.einsum(
            "bqhd,bkd->hbqk", q_b, band_k, preferred_element_type=jnp.float32
        ).reshape(per_dev, block_count, TILE_TOKENS, band, TILE_TOKENS)
        * score_scale
    )
    vert_allowed = vert_ok[:, :, None, :, None]
    neg = -jnp.inf
    band_top = jnp.max(jnp.where(band_allowed, band_scores, neg), axis=(3, 4))
    band_w = jnp.where(band_allowed, jnp.exp(band_scores - band_top[..., None, None]), 0.0)
    band_total = jnp.sum(band_w, axis=(3, 4))
    band_out = jnp.einsum(
        "hbqk,bkd->hbqd",
        band_w.astype(jnp.bfloat16).reshape(per_dev, block_count, TILE_TOKENS, band * TILE_TOKENS),
        band_v,
        preferred_element_type=jnp.float32,
    )
    band_out, band_total, band_top, vertical_kv = lax.optimization_barrier(
        (band_out, band_total, band_top, vertical_kv)
    )
    vert_k = vertical_kv[..., :HEAD_SIZE]
    vert_v = vertical_kv[..., HEAD_SIZE:]
    vert_scores = (
        jnp.einsum(
            "bqhd,hvkd->hbqvk", q_b, vert_k, preferred_element_type=jnp.float32
        )
        * score_scale
    )
    row_top = jnp.maximum(band_top, jnp.max(jnp.where(vert_allowed, vert_scores, neg), axis=(3, 4)))
    vert_w = jnp.where(vert_allowed, jnp.exp(vert_scores - row_top[..., None, None]), 0.0)
    band_scale = jnp.exp(band_top - row_top)
    row_total = band_total * band_scale + jnp.sum(vert_w, axis=(3, 4))
    blended = band_out * band_scale[..., None] + jnp.einsum(
        "hbqvk,hvkd->hbqd",
        vert_w.astype(jnp.bfloat16),
        vert_v,
        preferred_element_type=jnp.float32,
    )
    attended = (blended / row_total[..., None]).astype(jnp.bfloat16)
    attended, weight_cols = lax.optimization_barrier((attended, weight_cols))
    cz_count = lax.axis_size("cz")
    tiles = attended.transpose(1, 2, 0, 3).reshape(block_count, TILE_TOKENS, per_dev * HEAD_SIZE)
    spread_tiles = jnp.broadcast_to(tiles[None], (cz_count,) + tiles.shape).reshape(
        cz_count * block_count, TILE_TOKENS, per_dev * HEAD_SIZE
    )
    got = lax.all_to_all(spread_tiles, ("cz",) + HEAD_AXES, split_axis=0, concat_axis=0, tiled=True)
    attn_group = got.reshape(cz_count, head_count, TILE_TOKENS, per_dev * HEAD_SIZE)
    projected = jnp.einsum(
        "zhtd,hdn->ztn",
        attn_group,
        weight_cols.reshape(head_count, per_dev * HEAD_SIZE, -1),
        preferred_element_type=jnp.float32,
    ).astype(jnp.bfloat16).reshape(cz_count * TILE_TOKENS, -1)
    return lax.all_to_all(projected, "cz", split_axis=0, concat_axis=1, tiled=True)


def solution(mesh):
    ctx_count = mesh.shape["ctx"]
    cx_count = 4 if ctx_count % 4 == 0 else 1
    head_total = mesh.shape["head"]
    split_mesh = Mesh(
        mesh.devices.reshape(ctx_count // cx_count, cx_count, head_total // 2, 2),
        ("cz", "cx") + HEAD_AXES,
    )
    rows = P(("cz", "cx") + HEAD_AXES, None)
    placed = (rows, rows, rows, P(None, ("cz", "cx")), P(), P())
    return jax.shard_map(
        shards, mesh=split_mesh, in_specs=placed, out_specs=rows, check_vma=False
    )
```

```python
import numpy as np
import jax
import jax.numpy as jnp
from jax import lax
from jax.sharding import Mesh, PartitionSpec as P

HEAD_SIZE = 128
TILE_TOKENS = 128
CTX_AXES = ("cz", "cx")
HEAD_AXES = ("hy", "hc")


def passed_along(block, axes, distance):
    count = 1
    for axis in axes:
        count *= lax.axis_size(axis)
    route = [(i - distance, i) for i in range(count) if i - distance >= 0]
    return lax.ppermute(block, axes, route)


def shards(queries, keys, values, out_weight, vertical, slash):
    head_count = lax.axis_size("hy") * lax.axis_size("hc")
    head_index = lax.axis_index("hy") * lax.axis_size("hc") + lax.axis_index("hc")
    cx_count = lax.axis_size("cx")
    ctx_index = lax.axis_index("cz") * cx_count + lax.axis_index("cx")
    tok_rows = queries.shape[0]
    query_heads = vertical.shape[0]
    kv_count = keys.shape[1] // HEAD_SIZE
    group_width = query_heads // kv_count
    per_dev = query_heads // head_count
    ctx_rows = tok_rows * head_count
    block_count = ctx_rows // TILE_TOKENS
    slash_span = block_count
    band = slash_span + 1

    kv_of_dest = (np.arange(head_count) * per_dev) // group_width
    q_part = queries.reshape(tok_rows, head_count, per_dev * HEAD_SIZE)
    k_part = jnp.take(keys.reshape(tok_rows, kv_count, HEAD_SIZE), kv_of_dest, axis=1)
    v_part = jnp.take(values.reshape(tok_rows, kv_count, HEAD_SIZE), kv_of_dest, axis=1)
    send = jnp.concatenate([q_part, k_part, v_part], axis=2).reshape(tok_rows, -1)
    recv = lax.all_to_all(send, HEAD_AXES, split_axis=1, concat_axis=0, tiled=True)
    q_width = per_dev * HEAD_SIZE
    q_loc = recv[:, :q_width]
    kv_loc = recv[:, q_width:]
    kv_prev = passed_along(kv_loc, CTX_AXES, 1)
    part_rows = out_weight.shape[0] // head_count
    weight_part = lax.dynamic_slice_in_dim(out_weight, head_index * part_rows, part_rows, axis=0)
    weight_part = lax.all_gather(weight_part, "cz", axis=1, tiled=True)
    kv_loc, weight_part = lax.optimization_barrier((kv_loc, weight_part))
    weight_cols = lax.all_gather(weight_part, HEAD_AXES, axis=0, tiled=True)
    wide = jnp.concatenate([kv_prev, kv_loc], axis=0)

    my_heads = head_index * per_dev + jnp.arange(per_dev, dtype=jnp.int32)
    my_vertical = jnp.take(vertical, my_heads, axis=0)
    my_slash = jnp.take(slash, my_heads, axis=0)
    first_block = ctx_index * block_count
    local_vertical = my_vertical - first_block
    inside = (my_vertical >= 0) & (local_vertical >= 0) & (local_vertical < block_count)
    vertical_index = jnp.clip(local_vertical, 0, block_count - 1)
    kv_blocks = kv_loc.reshape(block_count, TILE_TOKENS, 2 * HEAD_SIZE)
    found = jnp.take(kv_blocks, vertical_index, axis=0)
    found = jnp.where(inside[:, :, None, None], found, jnp.zeros((), found.dtype))
    ctx_count = lax.axis_size("cz") * cx_count
    slot_shape = found.shape
    chunks = found.reshape(ctx_count, -1, TILE_TOKENS, 2 * HEAD_SIZE)
    gathered = lax.all_to_all(chunks, CTX_AXES, split_axis=0, concat_axis=0, tiled=True)
    reduced = jnp.sum(gathered.astype(jnp.float32), axis=0).astype(found.dtype)
    spread = jnp.broadcast_to(reduced[None], chunks.shape)
    vertical_kv = lax.all_to_all(spread, CTX_AXES, split_axis=0, concat_axis=0, tiled=True)
    vertical_kv = vertical_kv.reshape(slot_shape)
    vert_k = vertical_kv[..., :HEAD_SIZE]
    vert_v = vertical_kv[..., HEAD_SIZE:]

    band_kv = jnp.stack(
        [
            lax.slice_in_dim(
                wide, (b + block_count - slash_span) * TILE_TOKENS,
                (b + block_count + 1) * TILE_TOKENS, axis=0,
            )
            for b in range(block_count)
        ]
    )
    band_k = band_kv[..., :HEAD_SIZE]
    band_v = band_kv[..., HEAD_SIZE:]
    q_b = q_loc.reshape(block_count, TILE_TOKENS, per_dev, HEAD_SIZE)
    score_scale = HEAD_SIZE ** (-0.5)

    block_ids = first_block + jnp.arange(block_count, dtype=jnp.int32)
    offsets = slash_span - jnp.arange(band, dtype=jnp.int32)
    live_slash = my_slash >= 1
    slash_hit = jnp.any(
        (my_slash[:, None, :] == offsets[None, :, None]) & live_slash[:, None, :], axis=2
    )
    band_ok = (
        slash_hit[:, None, :]
        & (offsets[None, None, :] >= 1)
        & ((block_ids[:, None] - offsets[None, :]) >= 0)[None, :, :]
    )
    causal = jnp.tril(jnp.ones((TILE_TOKENS, TILE_TOKENS), dtype=bool))
    own_tile = (offsets == 0)[None, None, None, :, None] & causal[None, None, :, None, :]
    band_allowed = band_ok[:, :, None, :, None] | own_tile
    repeats = jnp.any(
        ((block_ids[None, :, None] - my_vertical[:, None, :])[:, :, :, None] == my_slash[:, None, None, :])
        & live_slash[:, None, None, :],
        axis=3,
    )
    vert_ok = (
        (my_vertical[:, None, :] >= 0)
        & (my_vertical[:, None, :] < block_ids[None, :, None])
        & jnp.logical_not(repeats)
    )

    band_scores = (
        jnp.einsum(
            "bqhd,bkd->hbqk", q_b, band_k, preferred_element_type=jnp.float32
        ).reshape(per_dev, block_count, TILE_TOKENS, band, TILE_TOKENS)
        * score_scale
    )
    vert_allowed = vert_ok[:, :, None, :, None]
    neg = -jnp.inf
    band_top = jnp.max(jnp.where(band_allowed, band_scores, neg), axis=(3, 4))
    band_w = jnp.where(band_allowed, jnp.exp(band_scores - band_top[..., None, None]), 0.0)
    band_total = jnp.sum(band_w, axis=(3, 4))
    band_out = jnp.einsum(
        "hbqk,bkd->hbqd",
        band_w.astype(jnp.bfloat16).reshape(per_dev, block_count, TILE_TOKENS, band * TILE_TOKENS),
        band_v,
        preferred_element_type=jnp.float32,
    )
    band_out, band_total, band_top, vertical_kv = lax.optimization_barrier(
        (band_out, band_total, band_top, vertical_kv)
    )
    vert_k = vertical_kv[..., :HEAD_SIZE]
    vert_v = vertical_kv[..., HEAD_SIZE:]
    vert_scores = (
        jnp.einsum(
            "bqhd,hvkd->hbqvk", q_b, vert_k, preferred_element_type=jnp.float32
        )
        * score_scale
    )
    row_top = jnp.maximum(band_top, jnp.max(jnp.where(vert_allowed, vert_scores, neg), axis=(3, 4)))
    vert_w = jnp.where(vert_allowed, jnp.exp(vert_scores - row_top[..., None, None]), 0.0)
    band_scale = jnp.exp(band_top - row_top)
    row_total = band_total * band_scale + jnp.sum(vert_w, axis=(3, 4))
    blended = band_out * band_scale[..., None] + jnp.einsum(
        "hbqvk,hvkd->hbqd",
        vert_w.astype(jnp.bfloat16),
        vert_v,
        preferred_element_type=jnp.float32,
    )
    attended = (blended / row_total[..., None]).astype(jnp.bfloat16)
    attended, weight_cols = lax.optimization_barrier((attended, weight_cols))
    cz_count = lax.axis_size("cx")
    tiles = attended.transpose(1, 2, 0, 3).reshape(block_count, TILE_TOKENS, per_dev * HEAD_SIZE)
    spread_tiles = jnp.broadcast_to(tiles[None], (cz_count,) + tiles.shape).reshape(
        cz_count * block_count, TILE_TOKENS, per_dev * HEAD_SIZE
    )
    got = lax.all_to_all(spread_tiles, ("cx",) + HEAD_AXES, split_axis=0, concat_axis=0, tiled=True)
    attn_group = got.reshape(cz_count, head_count, TILE_TOKENS, per_dev * HEAD_SIZE)
    projected = jnp.einsum(
        "zhtd,hdn->ztn",
        attn_group,
        weight_cols.reshape(head_count, per_dev * HEAD_SIZE, -1),
        preferred_element_type=jnp.float32,
    ).astype(jnp.bfloat16).reshape(cz_count * TILE_TOKENS, -1)
    out = lax.all_to_all(projected, "cx", split_axis=0, concat_axis=1, tiled=True)
    out = out.reshape(tok_rows, cx_count, lax.axis_size("cz"), -1).transpose(0, 2, 1, 3)
    return out.reshape(tok_rows, -1)


def solution(mesh):
    ctx_count = mesh.shape["ctx"]
    cx_count = 4 if ctx_count % 4 == 0 else 1
    head_total = mesh.shape["head"]
    split_mesh = Mesh(
        mesh.devices.reshape(ctx_count // cx_count, cx_count, head_total // 2, 2),
        ("cz", "cx") + HEAD_AXES,
    )
    rows = P(("cz", "cx") + HEAD_AXES, None)
    placed = (rows, rows, rows, P(None, ("cz", "cx")), P(), P())
    return jax.shard_map(
        shards, mesh=split_mesh, in_specs=placed, out_specs=rows, check_vma=False
    )
```

```python
import numpy as np
import jax
import jax.numpy as jnp
from jax import lax
from jax.sharding import Mesh, PartitionSpec as P

HEAD_SIZE = 128
TILE_TOKENS = 128
CTX_AXES = ("cz", "cx")
HEAD_AXES = ("hy", "hc")


def passed_along(block, axes, distance):
    count = 1
    for axis in axes:
        count *= lax.axis_size(axis)
    route = [(i - distance, i) for i in range(count) if i - distance >= 0]
    return lax.ppermute(block, axes, route)


def shards(queries, keys, values, out_weight, vertical, slash):
    head_count = lax.axis_size("hy") * lax.axis_size("hc")
    head_index = lax.axis_index("hy") * lax.axis_size("hc") + lax.axis_index("hc")
    cx_count = lax.axis_size("cx")
    ctx_index = lax.axis_index("cz") * cx_count + lax.axis_index("cx")
    tok_rows = queries.shape[0]
    query_heads = vertical.shape[0]
    kv_count = keys.shape[1] // HEAD_SIZE
    group_width = query_heads // kv_count
    per_dev = query_heads // head_count
    ctx_rows = tok_rows * head_count
    block_count = ctx_rows // TILE_TOKENS
    slash_span = block_count
    band = slash_span + 1

    kv_of_dest = (np.arange(head_count) * per_dev) // group_width
    q_part = queries.reshape(tok_rows, head_count, per_dev * HEAD_SIZE)
    k_part = jnp.take(keys.reshape(tok_rows, kv_count, HEAD_SIZE), kv_of_dest, axis=1)
    v_part = jnp.take(values.reshape(tok_rows, kv_count, HEAD_SIZE), kv_of_dest, axis=1)
    send = jnp.concatenate([q_part, k_part, v_part], axis=2).reshape(tok_rows, -1)
    recv = lax.all_to_all(send, HEAD_AXES, split_axis=1, concat_axis=0, tiled=True)
    q_width = per_dev * HEAD_SIZE
    q_loc = recv[:, :q_width]
    kv_loc = recv[:, q_width:]
    kv_prev = passed_along(kv_loc, CTX_AXES, 1)
    part_rows = out_weight.shape[0] // head_count
    weight_part = lax.dynamic_slice_in_dim(out_weight, head_index * part_rows, part_rows, axis=0)
    weight_part = lax.all_gather(weight_part, "cx", axis=1, tiled=True)
    kv_loc, weight_part = lax.optimization_barrier((kv_loc, weight_part))
    weight_cols = lax.all_gather(weight_part, HEAD_AXES, axis=0, tiled=True)
    wide = jnp.concatenate([kv_prev, kv_loc], axis=0)

    my_heads = head_index * per_dev + jnp.arange(per_dev, dtype=jnp.int32)
    my_vertical = jnp.take(vertical, my_heads, axis=0)
    my_slash = jnp.take(slash, my_heads, axis=0)
    first_block = ctx_index * block_count
    local_vertical = my_vertical - first_block
    inside = (my_vertical >= 0) & (local_vertical >= 0) & (local_vertical < block_count)
    vertical_index = jnp.clip(local_vertical, 0, block_count - 1)
    kv_blocks = kv_loc.reshape(block_count, TILE_TOKENS, 2 * HEAD_SIZE)
    found = jnp.take(kv_blocks, vertical_index, axis=0)
    found = jnp.where(inside[:, :, None, None], found, jnp.zeros((), found.dtype))
    ctx_count = lax.axis_size("cz") * cx_count
    slot_shape = found.shape
    chunks = found.reshape(ctx_count, -1, TILE_TOKENS, 2 * HEAD_SIZE)
    gathered = lax.all_to_all(chunks, CTX_AXES, split_axis=0, concat_axis=0, tiled=True)
    reduced = jnp.sum(gathered.astype(jnp.float32), axis=0).astype(found.dtype)
    spread = jnp.broadcast_to(reduced[None], chunks.shape)
    vertical_kv = lax.all_to_all(spread, CTX_AXES, split_axis=0, concat_axis=0, tiled=True)
    vertical_kv = vertical_kv.reshape(slot_shape)
    vert_k = vertical_kv[..., :HEAD_SIZE]
    vert_v = vertical_kv[..., HEAD_SIZE:]

    band_kv = jnp.stack(
        [
            lax.slice_in_dim(
                wide, (b + block_count - slash_span) * TILE_TOKENS,
                (b + block_count + 1) * TILE_TOKENS, axis=0,
            )
            for b in range(block_count)
        ]
    )
    band_k = band_kv[..., :HEAD_SIZE]
    band_v = band_kv[..., HEAD_SIZE:]
    q_b = q_loc.reshape(block_count, TILE_TOKENS, per_dev, HEAD_SIZE)
    score_scale = HEAD_SIZE ** (-0.5)

    block_ids = first_block + jnp.arange(block_count, dtype=jnp.int32)
    offsets = slash_span - jnp.arange(band, dtype=jnp.int32)
    live_slash = my_slash >= 1
    slash_hit = jnp.any(
        (my_slash[:, None, :] == offsets[None, :, None]) & live_slash[:, None, :], axis=2
    )
    band_ok = (
        slash_hit[:, None, :]
        & (offsets[None, None, :] >= 1)
        & ((block_ids[:, None] - offsets[None, :]) >= 0)[None, :, :]
    )
    causal = jnp.tril(jnp.ones((TILE_TOKENS, TILE_TOKENS), dtype=bool))
    own_tile = (offsets == 0)[None, None, None, :, None] & causal[None, None, :, None, :]
    band_allowed = band_ok[:, :, None, :, None] | own_tile
    repeats = jnp.any(
        ((block_ids[None, :, None] - my_vertical[:, None, :])[:, :, :, None] == my_slash[:, None, None, :])
        & live_slash[:, None, None, :],
        axis=3,
    )
    vert_ok = (
        (my_vertical[:, None, :] >= 0)
        & (my_vertical[:, None, :] < block_ids[None, :, None])
        & jnp.logical_not(repeats)
    )

    band_scores = (
        jnp.einsum(
            "bqhd,bkd->hbqk", q_b, band_k, preferred_element_type=jnp.float32
        ).reshape(per_dev, block_count, TILE_TOKENS, band, TILE_TOKENS)
        * score_scale
    )
    vert_allowed = vert_ok[:, :, None, :, None]
    neg = -jnp.inf
    band_top = jnp.max(jnp.where(band_allowed, band_scores, neg), axis=(3, 4))
    band_w = jnp.where(band_allowed, jnp.exp(band_scores - band_top[..., None, None]), 0.0)
    band_total = jnp.sum(band_w, axis=(3, 4))
    band_out = jnp.einsum(
        "hbqk,bkd->hbqd",
        band_w.astype(jnp.bfloat16).reshape(per_dev, block_count, TILE_TOKENS, band * TILE_TOKENS),
        band_v,
        preferred_element_type=jnp.float32,
    )
    band_out, band_total, band_top, vertical_kv = lax.optimization_barrier(
        (band_out, band_total, band_top, vertical_kv)
    )
    vert_k = vertical_kv[..., :HEAD_SIZE]
    vert_v = vertical_kv[..., HEAD_SIZE:]
    vert_scores = (
        jnp.einsum(
            "bqhd,hvkd->hbqvk", q_b, vert_k, preferred_element_type=jnp.float32
        )
        * score_scale
    )
    row_top = jnp.maximum(band_top, jnp.max(jnp.where(vert_allowed, vert_scores, neg), axis=(3, 4)))
    vert_w = jnp.where(vert_allowed, jnp.exp(vert_scores - row_top[..., None, None]), 0.0)
    band_scale = jnp.exp(band_top - row_top)
    row_total = band_total * band_scale + jnp.sum(vert_w, axis=(3, 4))
    blended = band_out * band_scale[..., None] + jnp.einsum(
        "hbqvk,hvkd->hbqd",
        vert_w.astype(jnp.bfloat16),
        vert_v,
        preferred_element_type=jnp.float32,
    )
    attended = (blended / row_total[..., None]).astype(jnp.bfloat16)
    attended, weight_cols = lax.optimization_barrier((attended, weight_cols))
    cz_count = lax.axis_size("cz")
    tiles = attended.transpose(1, 2, 0, 3).reshape(block_count, TILE_TOKENS, per_dev * HEAD_SIZE)
    spread_tiles = jnp.broadcast_to(tiles[None], (cz_count,) + tiles.shape).reshape(
        cz_count * block_count, TILE_TOKENS, per_dev * HEAD_SIZE
    )
    got = lax.all_to_all(spread_tiles, ("cz",) + HEAD_AXES, split_axis=0, concat_axis=0, tiled=True)
    attn_group = got.reshape(cz_count, head_count, TILE_TOKENS, per_dev * HEAD_SIZE)
    projected = jnp.einsum(
        "zhtd,hdn->ztn",
        attn_group,
        weight_cols.reshape(head_count, per_dev * HEAD_SIZE, -1),
        preferred_element_type=jnp.float32,
    ).astype(jnp.bfloat16).reshape(cz_count * TILE_TOKENS, -1)
    blocks = projected.reshape(cz_count, TILE_TOKENS, -1)
    cz_index = lax.axis_index("cz")
    pieces = []
    for shift in range(cz_count):
        outgoing = jnp.take(blocks, (cz_index + shift) % cz_count, axis=0)
        if shift == 0:
            pieces.append(outgoing)
            continue
        route = [(i, (i + shift) % cz_count) for i in range(cz_count)]
        pieces.append(lax.ppermute(outgoing, "cz", route))
    source_order = (cz_index - jnp.arange(cz_count)) % cz_count
    ordered = jnp.take(jnp.stack(pieces), jnp.argsort(source_order), axis=0)
    return ordered.transpose(1, 0, 2).reshape(TILE_TOKENS, -1)


def solution(mesh):
    ctx_count = mesh.shape["ctx"]
    cx_count = 4 if ctx_count % 4 == 0 else 1
    head_total = mesh.shape["head"]
    split_mesh = Mesh(
        mesh.devices.reshape(ctx_count // cx_count, cx_count, head_total // 2, 2),
        ("cz", "cx") + HEAD_AXES,
    )
    rows = P(("cz", "cx") + HEAD_AXES, None)
    placed = (rows, rows, rows, P(None, ("cz", "cx")), P(), P())
    return jax.shard_map(
        shards, mesh=split_mesh, in_specs=placed, out_specs=rows, check_vma=False
    )
```

```python
import numpy as np
import jax
import jax.numpy as jnp
from jax import lax
from jax.sharding import Mesh, PartitionSpec as P

HEAD_SIZE = 128
TILE_TOKENS = 128
CTX_AXES = ("cz", "cx")
HEAD_AXES = ("hy", "hc")


def passed_along(block, axes, distance):
    count = 1
    for axis in axes:
        count *= lax.axis_size(axis)
    route = [(i - distance, i) for i in range(count) if i - distance >= 0]
    return lax.ppermute(block, axes, route)


def shards(queries, keys, values, out_weight, vertical, slash):
    head_count = lax.axis_size("hy") * lax.axis_size("hc")
    head_index = lax.axis_index("hy") * lax.axis_size("hc") + lax.axis_index("hc")
    cx_count = lax.axis_size("cx")
    ctx_index = lax.axis_index("cz") * cx_count + lax.axis_index("cx")
    tok_rows = queries.shape[0]
    query_heads = vertical.shape[0]
    kv_count = keys.shape[1] // HEAD_SIZE
    group_width = query_heads // kv_count
    per_dev = query_heads // head_count
    ctx_rows = tok_rows * head_count
    block_count = ctx_rows // TILE_TOKENS
    slash_span = block_count
    band = slash_span + 1

    kv_of_dest = (np.arange(head_count) * per_dev) // group_width
    q_part = queries.reshape(tok_rows, head_count, per_dev * HEAD_SIZE)
    k_part = jnp.take(keys.reshape(tok_rows, kv_count, HEAD_SIZE), kv_of_dest, axis=1)
    v_part = jnp.take(values.reshape(tok_rows, kv_count, HEAD_SIZE), kv_of_dest, axis=1)
    send = jnp.concatenate([q_part, k_part, v_part], axis=2).reshape(tok_rows, -1)
    recv = lax.all_to_all(send, HEAD_AXES, split_axis=1, concat_axis=0, tiled=True)
    q_width = per_dev * HEAD_SIZE
    q_loc = recv[:, :q_width]
    kv_loc = recv[:, q_width:]
    kv_prev = passed_along(kv_loc, CTX_AXES, 1)
    part_rows = out_weight.shape[0] // head_count
    weight_part = lax.dynamic_slice_in_dim(out_weight, head_index * part_rows, part_rows, axis=0)
    weight_part = lax.all_gather(weight_part, "cx", axis=1, tiled=True)
    kv_loc, weight_part = lax.optimization_barrier((kv_loc, weight_part))
    weight_cols = lax.all_gather(weight_part, HEAD_AXES, axis=0, tiled=True)
    wide = jnp.concatenate([kv_prev, kv_loc], axis=0)

    my_heads = head_index * per_dev + jnp.arange(per_dev, dtype=jnp.int32)
    my_vertical = jnp.take(vertical, my_heads, axis=0)
    my_slash = jnp.take(slash, my_heads, axis=0)
    first_block = ctx_index * block_count
    local_vertical = my_vertical - first_block
    inside = (my_vertical >= 0) & (local_vertical >= 0) & (local_vertical < block_count)
    vertical_index = jnp.clip(local_vertical, 0, block_count - 1)
    kv_blocks = kv_loc.reshape(block_count, TILE_TOKENS, 2 * HEAD_SIZE)
    found = jnp.take(kv_blocks, vertical_index, axis=0)
    found = jnp.where(inside[:, :, None, None], found, jnp.zeros((), found.dtype))
    ctx_count = lax.axis_size("cz") * cx_count
    slot_shape = found.shape
    chunks = found.reshape(ctx_count, -1, TILE_TOKENS, 2 * HEAD_SIZE)
    gathered = lax.all_to_all(chunks, CTX_AXES, split_axis=0, concat_axis=0, tiled=True)
    reduced = jnp.sum(gathered.astype(jnp.float32), axis=0).astype(found.dtype)
    spread = jnp.broadcast_to(reduced[None], chunks.shape)
    vertical_kv = lax.all_to_all(spread, CTX_AXES, split_axis=0, concat_axis=0, tiled=True)
    vertical_kv = vertical_kv.reshape(slot_shape)
    vert_k = vertical_kv[..., :HEAD_SIZE]
    vert_v = vertical_kv[..., HEAD_SIZE:]

    band_kv = jnp.stack(
        [
            lax.slice_in_dim(
                wide, (b + block_count - slash_span) * TILE_TOKENS,
                (b + block_count + 1) * TILE_TOKENS, axis=0,
            )
            for b in range(block_count)
        ]
    )
    band_k = band_kv[..., :HEAD_SIZE]
    band_v = band_kv[..., HEAD_SIZE:]
    q_b = q_loc.reshape(block_count, TILE_TOKENS, per_dev, HEAD_SIZE)
    score_scale = HEAD_SIZE ** (-0.5)

    block_ids = first_block + jnp.arange(block_count, dtype=jnp.int32)
    offsets = slash_span - jnp.arange(band, dtype=jnp.int32)
    live_slash = my_slash >= 1
    slash_hit = jnp.any(
        (my_slash[:, None, :] == offsets[None, :, None]) & live_slash[:, None, :], axis=2
    )
    band_ok = (
        slash_hit[:, None, :]
        & (offsets[None, None, :] >= 1)
        & ((block_ids[:, None] - offsets[None, :]) >= 0)[None, :, :]
    )
    causal = jnp.tril(jnp.ones((TILE_TOKENS, TILE_TOKENS), dtype=bool))
    own_tile = (offsets == 0)[None, None, None, :, None] & causal[None, None, :, None, :]
    band_allowed = band_ok[:, :, None, :, None] | own_tile
    repeats = jnp.any(
        ((block_ids[None, :, None] - my_vertical[:, None, :])[:, :, :, None] == my_slash[:, None, None, :])
        & live_slash[:, None, None, :],
        axis=3,
    )
    vert_ok = (
        (my_vertical[:, None, :] >= 0)
        & (my_vertical[:, None, :] < block_ids[None, :, None])
        & jnp.logical_not(repeats)
    )

    band_scores = (
        jnp.einsum(
            "bqhd,bkd->hbqk", q_b, band_k, preferred_element_type=jnp.float32
        ).reshape(per_dev, block_count, TILE_TOKENS, band, TILE_TOKENS)
        * score_scale
    )
    vert_allowed = vert_ok[:, :, None, :, None]
    neg = -jnp.inf
    band_top = jnp.max(jnp.where(band_allowed, band_scores, neg), axis=(3, 4))
    band_w = jnp.where(band_allowed, jnp.exp(band_scores - band_top[..., None, None]), 0.0)
    band_total = jnp.sum(band_w, axis=(3, 4))
    band_out = jnp.einsum(
        "hbqk,bkd->hbqd",
        band_w.astype(jnp.bfloat16).reshape(per_dev, block_count, TILE_TOKENS, band * TILE_TOKENS),
        band_v,
        preferred_element_type=jnp.float32,
    )
    band_out, band_total, band_top, vertical_kv = lax.optimization_barrier(
        (band_out, band_total, band_top, vertical_kv)
    )
    vert_k = vertical_kv[..., :HEAD_SIZE]
    vert_v = vertical_kv[..., HEAD_SIZE:]
    vert_scores = (
        jnp.einsum(
            "bqhd,hvkd->hbqvk", q_b, vert_k, preferred_element_type=jnp.float32
        )
        * score_scale
    )
    row_top = jnp.maximum(band_top, jnp.max(jnp.where(vert_allowed, vert_scores, neg), axis=(3, 4)))
    vert_w = jnp.where(vert_allowed, jnp.exp(vert_scores - row_top[..., None, None]), 0.0)
    band_scale = jnp.exp(band_top - row_top)
    row_total = band_total * band_scale + jnp.sum(vert_w, axis=(3, 4))
    blended = band_out * band_scale[..., None] + jnp.einsum(
        "hbqvk,hvkd->hbqd",
        vert_w.astype(jnp.bfloat16),
        vert_v,
        preferred_element_type=jnp.float32,
    )
    attended = (blended / row_total[..., None]).astype(jnp.bfloat16)
    attended, weight_cols = lax.optimization_barrier((attended, weight_cols))
    cz_count = lax.axis_size("cz")
    tiles = attended.transpose(1, 2, 0, 3).reshape(block_count, TILE_TOKENS, per_dev * HEAD_SIZE)
    spread_tiles = jnp.broadcast_to(
        tiles[:, None], (block_count, cz_count) + tiles.shape[1:]
    ).reshape(block_count * cz_count, TILE_TOKENS, per_dev * HEAD_SIZE)
    got = lax.all_to_all(spread_tiles, HEAD_AXES + ("cz",), split_axis=0, concat_axis=0, tiled=True)
    attn_group = got.reshape(head_count, cz_count, TILE_TOKENS, per_dev * HEAD_SIZE)
    projected = jnp.einsum(
        "hztd,hdn->ztn",
        attn_group,
        weight_cols.reshape(head_count, per_dev * HEAD_SIZE, -1),
        preferred_element_type=jnp.float32,
    ).astype(jnp.bfloat16).reshape(cz_count * TILE_TOKENS, -1)
    return lax.all_to_all(projected, "cz", split_axis=0, concat_axis=1, tiled=True)


def solution(mesh):
    ctx_count = mesh.shape["ctx"]
    cx_count = 4 if ctx_count % 4 == 0 else 1
    head_total = mesh.shape["head"]
    split_mesh = Mesh(
        mesh.devices.reshape(ctx_count // cx_count, cx_count, head_total // 2, 2),
        ("cz", "cx") + HEAD_AXES,
    )
    rows = P(("cz", "cx") + HEAD_AXES, None)
    placed = (rows, rows, rows, P(None, ("cz", "cx")), P(), P())
    return jax.shard_map(
        shards, mesh=split_mesh, in_specs=placed, out_specs=rows, check_vma=False
    )
```

```python
import numpy as np
import jax
import jax.numpy as jnp
from jax import lax
from jax.sharding import Mesh, PartitionSpec as P

HEAD_SIZE = 128
TILE_TOKENS = 128
CTX_AXES = ("cz", "cx")
HEAD_AXES = ("hy", "hc")


def passed_along(block, axes, distance):
    count = 1
    for axis in axes:
        count *= lax.axis_size(axis)
    route = [(i - distance, i) for i in range(count) if i - distance >= 0]
    return lax.ppermute(block, axes, route)


def shards(queries, keys, values, out_weight, vertical, slash):
    head_count = lax.axis_size("hy") * lax.axis_size("hc")
    head_index = lax.axis_index("hy") * lax.axis_size("hc") + lax.axis_index("hc")
    cx_count = lax.axis_size("cx")
    ctx_index = lax.axis_index("cz") * cx_count + lax.axis_index("cx")
    tok_rows = queries.shape[0]
    query_heads = vertical.shape[0]
    kv_count = keys.shape[1] // HEAD_SIZE
    group_width = query_heads // kv_count
    per_dev = query_heads // head_count
    ctx_rows = tok_rows * head_count
    block_count = ctx_rows // TILE_TOKENS
    slash_span = block_count
    band = slash_span + 1

    kv_of_dest = (np.arange(head_count) * per_dev) // group_width
    q_part = queries.reshape(tok_rows, head_count, per_dev * HEAD_SIZE)
    k_part = jnp.take(keys.reshape(tok_rows, kv_count, HEAD_SIZE), kv_of_dest, axis=1)
    v_part = jnp.take(values.reshape(tok_rows, kv_count, HEAD_SIZE), kv_of_dest, axis=1)
    send = jnp.concatenate([q_part, k_part, v_part], axis=2).reshape(tok_rows, -1)
    recv = lax.all_to_all(send, HEAD_AXES, split_axis=1, concat_axis=0, tiled=True)
    q_width = per_dev * HEAD_SIZE
    q_loc = recv[:, :q_width]
    kv_loc = recv[:, q_width:]
    kv_prev = passed_along(kv_loc, CTX_AXES, 1)
    part_rows = out_weight.shape[0] // head_count
    weight_part = lax.dynamic_slice_in_dim(out_weight, head_index * part_rows, part_rows, axis=0)
    weight_part = lax.all_gather(weight_part, "cx", axis=1, tiled=True)
    kv_loc, weight_part = lax.optimization_barrier((kv_loc, weight_part))
    weight_cols = lax.all_gather(weight_part, HEAD_AXES, axis=0, tiled=True)
    wide = jnp.concatenate([kv_prev, kv_loc], axis=0)

    my_heads = head_index * per_dev + jnp.arange(per_dev, dtype=jnp.int32)
    my_vertical = jnp.take(vertical, my_heads, axis=0)
    my_slash = jnp.take(slash, my_heads, axis=0)
    first_block = ctx_index * block_count
    local_vertical = my_vertical - first_block
    inside = (my_vertical >= 0) & (local_vertical >= 0) & (local_vertical < block_count)
    vertical_index = jnp.clip(local_vertical, 0, block_count - 1)
    kv_blocks = kv_loc.reshape(block_count, TILE_TOKENS, 2 * HEAD_SIZE)
    found = jnp.take(kv_blocks, vertical_index, axis=0)
    found = jnp.where(inside[:, :, None, None], found, jnp.zeros((), found.dtype))
    ctx_count = lax.axis_size("cz") * cx_count
    slot_shape = found.shape
    slot_count = found.shape[0] * found.shape[1]
    per_relay = slot_count // ctx_count

    def spread_back(reduced):
        spread = jnp.broadcast_to(reduced[None], (ctx_count,) + reduced.shape)
        return lax.all_to_all(spread, CTX_AXES, split_axis=0, concat_axis=0, tiled=True)

    def general_path(found):
        chunks = found.reshape(ctx_count, per_relay, TILE_TOKENS, 2 * HEAD_SIZE)
        gathered = lax.all_to_all(chunks, CTX_AXES, split_axis=0, concat_axis=0, tiled=True)
        reduced = jnp.sum(gathered.astype(jnp.float32), axis=0).astype(found.dtype)
        return spread_back(reduced).reshape(slot_shape)

    def owners_of(tiles):
        return jnp.where(tiles >= 0, tiles // block_count, ctx_count)

    def fast_path(found):
        owner = owners_of(my_vertical.reshape(-1))
        order = jnp.argsort(owner, stable=True)
        sorted_owner = jnp.take(owner, order)
        flat = found.reshape(slot_count, TILE_TOKENS, 2 * HEAD_SIZE)
        pos = jnp.arange(ctx_count)[:, None] + ctx_count * jnp.arange(per_relay)[None, :]
        mine = jnp.take(sorted_owner, pos) == ctx_index
        pick = jnp.sum(jnp.where(mine, jnp.take(order, pos), 0), axis=1)
        outgoing = jnp.where(jnp.any(mine, axis=1)[:, None, None], jnp.take(flat, pick, axis=0), 0)
        incoming = lax.all_to_all(outgoing[:, None], CTX_AXES, split_axis=0, concat_axis=0, tiled=True)
        my_owners = jnp.take(sorted_owner, ctx_index + ctx_count * jnp.arange(per_relay))
        reduced = jnp.take(incoming[:, 0], jnp.clip(my_owners, 0, ctx_count - 1), axis=0)
        reduced = jnp.where((my_owners < ctx_count)[:, None, None], reduced, 0).astype(found.dtype)
        by_pos = spread_back(reduced).transpose(1, 0, 2, 3).reshape(slot_count, TILE_TOKENS, -1)
        return jnp.take(by_pos, jnp.argsort(order), axis=0).reshape(slot_shape)

    all_owner = owners_of(vertical.reshape(head_count, -1))
    owner_load = jnp.sum(
        all_owner[:, :, None] == jnp.arange(ctx_count, dtype=all_owner.dtype)[None, None, :], axis=1
    )

    band_kv = jnp.stack(
        [
            lax.slice_in_dim(
                wide, (b + block_count - slash_span) * TILE_TOKENS,
                (b + block_count + 1) * TILE_TOKENS, axis=0,
            )
            for b in range(block_count)
        ]
    )
    band_k = band_kv[..., :HEAD_SIZE]
    band_v = band_kv[..., HEAD_SIZE:]
    q_b = q_loc.reshape(block_count, TILE_TOKENS, per_dev, HEAD_SIZE)
    score_scale = HEAD_SIZE ** (-0.5)

    block_ids = first_block + jnp.arange(block_count, dtype=jnp.int32)
    offsets = slash_span - jnp.arange(band, dtype=jnp.int32)
    live_slash = my_slash >= 1
    slash_hit = jnp.any(
        (my_slash[:, None, :] == offsets[None, :, None]) & live_slash[:, None, :], axis=2
    )
    band_ok = (
        slash_hit[:, None, :]
        & (offsets[None, None, :] >= 1)
        & ((block_ids[:, None] - offsets[None, :]) >= 0)[None, :, :]
    )
    causal = jnp.tril(jnp.ones((TILE_TOKENS, TILE_TOKENS), dtype=bool))
    own_tile = (offsets == 0)[None, None, None, :, None] & causal[None, None, :, None, :]
    band_allowed = band_ok[:, :, None, :, None] | own_tile
    repeats = jnp.any(
        ((block_ids[None, :, None] - my_vertical[:, None, :])[:, :, :, None] == my_slash[:, None, None, :])
        & live_slash[:, None, None, :],
        axis=3,
    )
    vert_ok = (
        (my_vertical[:, None, :] >= 0)
        & (my_vertical[:, None, :] < block_ids[None, :, None])
        & jnp.logical_not(repeats)
    )

    vert_allowed = vert_ok[:, :, None, :, None]
    neg = -jnp.inf

    def band_part():
        band_scores = (
            jnp.einsum(
                "bqhd,bkd->hbqk", q_b, band_k, preferred_element_type=jnp.float32
            ).reshape(per_dev, block_count, TILE_TOKENS, band, TILE_TOKENS)
            * score_scale
        )
        band_top = jnp.max(jnp.where(band_allowed, band_scores, neg), axis=(3, 4))
        band_w = jnp.where(band_allowed, jnp.exp(band_scores - band_top[..., None, None]), 0.0)
        band_total = jnp.sum(band_w, axis=(3, 4))
        band_out = jnp.einsum(
            "hbqk,bkd->hbqd",
            band_w.astype(jnp.bfloat16).reshape(per_dev, block_count, TILE_TOKENS, band * TILE_TOKENS),
            band_v,
            preferred_element_type=jnp.float32,
        )
        return band_out, band_total, band_top

    vertical_kv, band_out, band_total, band_top = lax.cond(
        jnp.max(owner_load) <= ctx_count,
        lambda f: (fast_path(f),) + band_part(),
        lambda f: (general_path(f),) + band_part(),
        found,
    )
    vert_k = vertical_kv[..., :HEAD_SIZE]
    vert_v = vertical_kv[..., HEAD_SIZE:]
    vert_scores = (
        jnp.einsum(
            "bqhd,hvkd->hbqvk", q_b, vert_k, preferred_element_type=jnp.float32
        )
        * score_scale
    )
    row_top = jnp.maximum(band_top, jnp.max(jnp.where(vert_allowed, vert_scores, neg), axis=(3, 4)))
    vert_w = jnp.where(vert_allowed, jnp.exp(vert_scores - row_top[..., None, None]), 0.0)
    band_scale = jnp.exp(band_top - row_top)
    row_total = band_total * band_scale + jnp.sum(vert_w, axis=(3, 4))
    blended = band_out * band_scale[..., None] + jnp.einsum(
        "hbqvk,hvkd->hbqd",
        vert_w.astype(jnp.bfloat16),
        vert_v,
        preferred_element_type=jnp.float32,
    )
    attended = (blended / row_total[..., None]).astype(jnp.bfloat16)
    attended, weight_cols = lax.optimization_barrier((attended, weight_cols))
    cz_count = lax.axis_size("cz")
    tiles = attended.transpose(1, 2, 0, 3).reshape(block_count, TILE_TOKENS, per_dev * HEAD_SIZE)
    spread_tiles = jnp.broadcast_to(
        tiles[:, None], (block_count, cz_count) + tiles.shape[1:]
    ).reshape(block_count * cz_count, TILE_TOKENS, per_dev * HEAD_SIZE)
    got = lax.all_to_all(spread_tiles, HEAD_AXES + ("cz",), split_axis=0, concat_axis=0, tiled=True)
    attn_group = got.reshape(head_count, cz_count, TILE_TOKENS, per_dev * HEAD_SIZE)
    projected = jnp.einsum(
        "hztd,hdn->ztn",
        attn_group,
        weight_cols.reshape(head_count, per_dev * HEAD_SIZE, -1),
        preferred_element_type=jnp.float32,
    ).astype(jnp.bfloat16).reshape(cz_count * TILE_TOKENS, -1)
    return lax.all_to_all(projected, "cz", split_axis=0, concat_axis=1, tiled=True)


def solution(mesh):
    ctx_count = mesh.shape["ctx"]
    cx_count = 4 if ctx_count % 4 == 0 else 1
    head_total = mesh.shape["head"]
    split_mesh = Mesh(
        mesh.devices.reshape(ctx_count // cx_count, cx_count, head_total // 2, 2),
        ("cz", "cx") + HEAD_AXES,
    )
    rows = P(("cz", "cx") + HEAD_AXES, None)
    placed = (rows, rows, rows, P(None, ("cz", "cx")), P(), P())
    return jax.shard_map(
        shards, mesh=split_mesh, in_specs=placed, out_specs=rows, check_vma=False
    )
```

```python
import numpy as np
import jax
import jax.numpy as jnp
from jax import lax
from jax.sharding import Mesh, PartitionSpec as P

HEAD_SIZE = 128
TILE_TOKENS = 128
CTX_AXES = ("cz", "cx")
HEAD_AXES = ("hy", "hc")


def passed_along(block, axes, distance):
    count = 1
    for axis in axes:
        count *= lax.axis_size(axis)
    route = [(i - distance, i) for i in range(count) if i - distance >= 0]
    return lax.ppermute(block, axes, route)


def shards(queries, keys, values, out_weight, vertical, slash):
    head_count = lax.axis_size("hy") * lax.axis_size("hc")
    head_index = lax.axis_index("hy") * lax.axis_size("hc") + lax.axis_index("hc")
    cx_count = lax.axis_size("cx")
    ctx_index = lax.axis_index("cz") * cx_count + lax.axis_index("cx")
    tok_rows = queries.shape[0]
    query_heads = vertical.shape[0]
    kv_count = keys.shape[1] // HEAD_SIZE
    group_width = query_heads // kv_count
    per_dev = query_heads // head_count
    ctx_rows = tok_rows * head_count
    block_count = ctx_rows // TILE_TOKENS
    slash_span = block_count
    band = slash_span + 1

    kv_of_dest = (np.arange(head_count) * per_dev) // group_width
    q_part = queries.reshape(tok_rows, head_count, per_dev * HEAD_SIZE)
    k_part = jnp.take(keys.reshape(tok_rows, kv_count, HEAD_SIZE), kv_of_dest, axis=1)
    v_part = jnp.take(values.reshape(tok_rows, kv_count, HEAD_SIZE), kv_of_dest, axis=1)
    send = jnp.concatenate([q_part, k_part, v_part], axis=2).reshape(tok_rows, -1)
    recv = lax.all_to_all(send, HEAD_AXES, split_axis=1, concat_axis=0, tiled=True)
    q_width = per_dev * HEAD_SIZE
    q_loc = recv[:, :q_width]
    kv_loc = recv[:, q_width:]
    kv_prev = passed_along(kv_loc, CTX_AXES, 1)
    part_rows = out_weight.shape[0] // head_count
    weight_part = lax.dynamic_slice_in_dim(out_weight, head_index * part_rows, part_rows, axis=0)
    cx_index = lax.axis_index("cx")
    w_pieces = [weight_part]
    for shift in range(1, cx_count):
        route = [(i, (i + shift) % cx_count) for i in range(cx_count)]
        w_pieces.append(lax.ppermute(weight_part, "cx", route))
    w_source = (cx_index - jnp.arange(cx_count)) % cx_count
    w_sorted = jnp.take(jnp.stack(w_pieces), jnp.argsort(w_source), axis=0)
    weight_part = w_sorted.transpose(1, 0, 2).reshape(part_rows, -1)
    kv_loc, weight_part = lax.optimization_barrier((kv_loc, weight_part))
    weight_cols = lax.all_gather(weight_part, HEAD_AXES, axis=0, tiled=True)
    wide = jnp.concatenate([kv_prev, kv_loc], axis=0)

    my_heads = head_index * per_dev + jnp.arange(per_dev, dtype=jnp.int32)
    my_vertical = jnp.take(vertical, my_heads, axis=0)
    my_slash = jnp.take(slash, my_heads, axis=0)
    first_block = ctx_index * block_count
    local_vertical = my_vertical - first_block
    inside = (my_vertical >= 0) & (local_vertical >= 0) & (local_vertical < block_count)
    vertical_index = jnp.clip(local_vertical, 0, block_count - 1)
    kv_blocks = kv_loc.reshape(block_count, TILE_TOKENS, 2 * HEAD_SIZE)
    found = jnp.take(kv_blocks, vertical_index, axis=0)
    found = jnp.where(inside[:, :, None, None], found, jnp.zeros((), found.dtype))
    ctx_count = lax.axis_size("cz") * cx_count
    slot_shape = found.shape
    chunks = found.reshape(ctx_count, -1, TILE_TOKENS, 2 * HEAD_SIZE)
    gathered = lax.all_to_all(chunks, CTX_AXES, split_axis=0, concat_axis=0, tiled=True)
    reduced = jnp.sum(gathered.astype(jnp.float32), axis=0).astype(found.dtype)
    spread = jnp.broadcast_to(reduced[None], chunks.shape)
    vertical_kv = lax.all_to_all(spread, CTX_AXES, split_axis=0, concat_axis=0, tiled=True)
    vertical_kv = vertical_kv.reshape(slot_shape)
    vert_k = vertical_kv[..., :HEAD_SIZE]
    vert_v = vertical_kv[..., HEAD_SIZE:]

    band_kv = jnp.stack(
        [
            lax.slice_in_dim(
                wide, (b + block_count - slash_span) * TILE_TOKENS,
                (b + block_count + 1) * TILE_TOKENS, axis=0,
            )
            for b in range(block_count)
        ]
    )
    band_k = band_kv[..., :HEAD_SIZE]
    band_v = band_kv[..., HEAD_SIZE:]
    q_b = q_loc.reshape(block_count, TILE_TOKENS, per_dev, HEAD_SIZE)
    score_scale = HEAD_SIZE ** (-0.5)

    block_ids = first_block + jnp.arange(block_count, dtype=jnp.int32)
    offsets = slash_span - jnp.arange(band, dtype=jnp.int32)
    live_slash = my_slash >= 1
    slash_hit = jnp.any(
        (my_slash[:, None, :] == offsets[None, :, None]) & live_slash[:, None, :], axis=2
    )
    band_ok = (
        slash_hit[:, None, :]
        & (offsets[None, None, :] >= 1)
        & ((block_ids[:, None] - offsets[None, :]) >= 0)[None, :, :]
    )
    causal = jnp.tril(jnp.ones((TILE_TOKENS, TILE_TOKENS), dtype=bool))
    own_tile = (offsets == 0)[None, None, None, :, None] & causal[None, None, :, None, :]
    band_allowed = band_ok[:, :, None, :, None] | own_tile
    repeats = jnp.any(
        ((block_ids[None, :, None] - my_vertical[:, None, :])[:, :, :, None] == my_slash[:, None, None, :])
        & live_slash[:, None, None, :],
        axis=3,
    )
    vert_ok = (
        (my_vertical[:, None, :] >= 0)
        & (my_vertical[:, None, :] < block_ids[None, :, None])
        & jnp.logical_not(repeats)
    )

    band_scores = (
        jnp.einsum(
            "bqhd,bkd->hbqk", q_b, band_k, preferred_element_type=jnp.float32
        ).reshape(per_dev, block_count, TILE_TOKENS, band, TILE_TOKENS)
        * score_scale
    )
    vert_allowed = vert_ok[:, :, None, :, None]
    neg = -jnp.inf
    band_top = jnp.max(jnp.where(band_allowed, band_scores, neg), axis=(3, 4))
    band_w = jnp.where(band_allowed, jnp.exp(band_scores - band_top[..., None, None]), 0.0)
    band_total = jnp.sum(band_w, axis=(3, 4))
    band_out = jnp.einsum(
        "hbqk,bkd->hbqd",
        band_w.astype(jnp.bfloat16).reshape(per_dev, block_count, TILE_TOKENS, band * TILE_TOKENS),
        band_v,
        preferred_element_type=jnp.float32,
    )
    band_out, band_total, band_top, vertical_kv = lax.optimization_barrier(
        (band_out, band_total, band_top, vertical_kv)
    )
    vert_k = vertical_kv[..., :HEAD_SIZE]
    vert_v = vertical_kv[..., HEAD_SIZE:]
    vert_scores = (
        jnp.einsum(
            "bqhd,hvkd->hbqvk", q_b, vert_k, preferred_element_type=jnp.float32
        )
        * score_scale
    )
    row_top = jnp.maximum(band_top, jnp.max(jnp.where(vert_allowed, vert_scores, neg), axis=(3, 4)))
    vert_w = jnp.where(vert_allowed, jnp.exp(vert_scores - row_top[..., None, None]), 0.0)
    band_scale = jnp.exp(band_top - row_top)
    row_total = band_total * band_scale + jnp.sum(vert_w, axis=(3, 4))
    blended = band_out * band_scale[..., None] + jnp.einsum(
        "hbqvk,hvkd->hbqd",
        vert_w.astype(jnp.bfloat16),
        vert_v,
        preferred_element_type=jnp.float32,
    )
    attended = (blended / row_total[..., None]).astype(jnp.bfloat16)
    attended, weight_cols = lax.optimization_barrier((attended, weight_cols))
    cz_count = lax.axis_size("cz")
    tiles = attended.transpose(1, 2, 0, 3).reshape(block_count, TILE_TOKENS, per_dev * HEAD_SIZE)
    spread_tiles = jnp.broadcast_to(
        tiles[:, None], (block_count, cz_count) + tiles.shape[1:]
    ).reshape(block_count * cz_count, TILE_TOKENS, per_dev * HEAD_SIZE)
    got = lax.all_to_all(spread_tiles, HEAD_AXES + ("cz",), split_axis=0, concat_axis=0, tiled=True)
    attn_group = got.reshape(head_count, cz_count, TILE_TOKENS, per_dev * HEAD_SIZE)
    projected = jnp.einsum(
        "hztd,hdn->ztn",
        attn_group,
        weight_cols.reshape(head_count, per_dev * HEAD_SIZE, -1),
        preferred_element_type=jnp.float32,
    ).astype(jnp.bfloat16).reshape(cz_count * TILE_TOKENS, -1)
    return lax.all_to_all(projected, "cz", split_axis=0, concat_axis=1, tiled=True)


def solution(mesh):
    ctx_count = mesh.shape["ctx"]
    cx_count = 4 if ctx_count % 4 == 0 else 1
    head_total = mesh.shape["head"]
    split_mesh = Mesh(
        mesh.devices.reshape(ctx_count // cx_count, cx_count, head_total // 2, 2),
        ("cz", "cx") + HEAD_AXES,
    )
    rows = P(("cz", "cx") + HEAD_AXES, None)
    placed = (rows, rows, rows, P(None, ("cz", "cx")), P(), P())
    return jax.shard_map(
        shards, mesh=split_mesh, in_specs=placed, out_specs=rows, check_vma=False
    )
```

```python
import numpy as np
import jax
import jax.numpy as jnp
from jax import lax
from jax.sharding import Mesh, PartitionSpec as P

HEAD_SIZE = 128
TILE_TOKENS = 128
CTX_AXES = ("cz", "cx")
HEAD_AXES = ("hy", "hc")


def passed_along(block, axes, distance):
    count = 1
    for axis in axes:
        count *= lax.axis_size(axis)
    route = [(i - distance, i) for i in range(count) if i - distance >= 0]
    return lax.ppermute(block, axes, route)


def shards(queries, keys, values, out_weight, vertical, slash):
    head_count = lax.axis_size("hy") * lax.axis_size("hc")
    head_index = lax.axis_index("hy") * lax.axis_size("hc") + lax.axis_index("hc")
    cx_count = lax.axis_size("cx")
    ctx_index = lax.axis_index("cz") * cx_count + lax.axis_index("cx")
    tok_rows = queries.shape[0]
    query_heads = vertical.shape[0]
    kv_count = keys.shape[1] // HEAD_SIZE
    group_width = query_heads // kv_count
    per_dev = query_heads // head_count
    ctx_rows = tok_rows * head_count
    block_count = ctx_rows // TILE_TOKENS
    slash_span = block_count
    band = slash_span + 1

    kv_of_dest = (np.arange(head_count) * per_dev) // group_width
    q_part = queries.reshape(tok_rows, head_count, per_dev * HEAD_SIZE)
    k_part = jnp.take(keys.reshape(tok_rows, kv_count, HEAD_SIZE), kv_of_dest, axis=1)
    v_part = jnp.take(values.reshape(tok_rows, kv_count, HEAD_SIZE), kv_of_dest, axis=1)
    send = jnp.concatenate([q_part, k_part, v_part], axis=2).reshape(tok_rows, -1)
    recv = lax.all_to_all(send, HEAD_AXES, split_axis=1, concat_axis=0, tiled=True)
    q_width = per_dev * HEAD_SIZE
    q_loc = recv[:, :q_width]
    kv_loc = recv[:, q_width:]
    core_index = lax.axis_index("hc")
    core_count = lax.axis_size("hc")
    half_tok = ctx_rows // core_count
    prev_mine = passed_along(
        lax.dynamic_slice_in_dim(kv_loc, core_index * half_tok, half_tok, axis=0), CTX_AXES, 1
    )
    prev_other = lax.ppermute(prev_mine, "hc", [(i, (i + 1) % core_count) for i in range(core_count)])
    prev_halves = jnp.stack([prev_mine, prev_other])
    kv_prev = jnp.take(prev_halves, (jnp.arange(core_count) + core_index) % core_count, axis=0)
    kv_prev = kv_prev.reshape(ctx_rows, -1)
    part_rows = out_weight.shape[0] // head_count
    weight_part = lax.dynamic_slice_in_dim(out_weight, head_index * part_rows, part_rows, axis=0)
    weight_part = lax.all_gather(weight_part, "cx", axis=1, tiled=True)
    kv_loc, weight_part = lax.optimization_barrier((kv_loc, weight_part))
    weight_cols = lax.all_gather(weight_part, HEAD_AXES, axis=0, tiled=True)
    wide = jnp.concatenate([kv_prev, kv_loc], axis=0)

    my_heads = head_index * per_dev + jnp.arange(per_dev, dtype=jnp.int32)
    my_vertical = jnp.take(vertical, my_heads, axis=0)
    my_slash = jnp.take(slash, my_heads, axis=0)
    first_block = ctx_index * block_count
    local_vertical = my_vertical - first_block
    inside = (my_vertical >= 0) & (local_vertical >= 0) & (local_vertical < block_count)
    vertical_index = jnp.clip(local_vertical, 0, block_count - 1)
    kv_blocks = kv_loc.reshape(block_count, TILE_TOKENS, 2 * HEAD_SIZE)
    found = jnp.take(kv_blocks, vertical_index, axis=0)
    found = jnp.where(inside[:, :, None, None], found, jnp.zeros((), found.dtype))
    ctx_count = lax.axis_size("cz") * cx_count
    slot_shape = found.shape
    chunks = found.reshape(ctx_count, -1, TILE_TOKENS, 2 * HEAD_SIZE)
    gathered = lax.all_to_all(chunks, CTX_AXES, split_axis=0, concat_axis=0, tiled=True)
    reduced = jnp.sum(gathered.astype(jnp.float32), axis=0).astype(found.dtype)
    spread = jnp.broadcast_to(reduced[None], chunks.shape)
    vertical_kv = lax.all_to_all(spread, CTX_AXES, split_axis=0, concat_axis=0, tiled=True)
    vertical_kv = vertical_kv.reshape(slot_shape)
    vert_k = vertical_kv[..., :HEAD_SIZE]
    vert_v = vertical_kv[..., HEAD_SIZE:]

    band_kv = jnp.stack(
        [
            lax.slice_in_dim(
                wide, (b + block_count - slash_span) * TILE_TOKENS,
                (b + block_count + 1) * TILE_TOKENS, axis=0,
            )
            for b in range(block_count)
        ]
    )
    band_k = band_kv[..., :HEAD_SIZE]
    band_v = band_kv[..., HEAD_SIZE:]
    q_b = q_loc.reshape(block_count, TILE_TOKENS, per_dev, HEAD_SIZE)
    score_scale = HEAD_SIZE ** (-0.5)

    block_ids = first_block + jnp.arange(block_count, dtype=jnp.int32)
    offsets = slash_span - jnp.arange(band, dtype=jnp.int32)
    live_slash = my_slash >= 1
    slash_hit = jnp.any(
        (my_slash[:, None, :] == offsets[None, :, None]) & live_slash[:, None, :], axis=2
    )
    band_ok = (
        slash_hit[:, None, :]
        & (offsets[None, None, :] >= 1)
        & ((block_ids[:, None] - offsets[None, :]) >= 0)[None, :, :]
    )
    causal = jnp.tril(jnp.ones((TILE_TOKENS, TILE_TOKENS), dtype=bool))
    own_tile = (offsets == 0)[None, None, None, :, None] & causal[None, None, :, None, :]
    band_allowed = band_ok[:, :, None, :, None] | own_tile
    repeats = jnp.any(
        ((block_ids[None, :, None] - my_vertical[:, None, :])[:, :, :, None] == my_slash[:, None, None, :])
        & live_slash[:, None, None, :],
        axis=3,
    )
    vert_ok = (
        (my_vertical[:, None, :] >= 0)
        & (my_vertical[:, None, :] < block_ids[None, :, None])
        & jnp.logical_not(repeats)
    )

    band_scores = (
        jnp.einsum(
            "bqhd,bkd->hbqk", q_b, band_k, preferred_element_type=jnp.float32
        ).reshape(per_dev, block_count, TILE_TOKENS, band, TILE_TOKENS)
        * score_scale
    )
    vert_allowed = vert_ok[:, :, None, :, None]
    neg = -jnp.inf
    band_top = jnp.max(jnp.where(band_allowed, band_scores, neg), axis=(3, 4))
    band_w = jnp.where(band_allowed, jnp.exp(band_scores - band_top[..., None, None]), 0.0)
    band_total = jnp.sum(band_w, axis=(3, 4))
    band_out = jnp.einsum(
        "hbqk,bkd->hbqd",
        band_w.astype(jnp.bfloat16).reshape(per_dev, block_count, TILE_TOKENS, band * TILE_TOKENS),
        band_v,
        preferred_element_type=jnp.float32,
    )
    band_out, band_total, band_top, vertical_kv = lax.optimization_barrier(
        (band_out, band_total, band_top, vertical_kv)
    )
    vert_k = vertical_kv[..., :HEAD_SIZE]
    vert_v = vertical_kv[..., HEAD_SIZE:]
    vert_scores = (
        jnp.einsum(
            "bqhd,hvkd->hbqvk", q_b, vert_k, preferred_element_type=jnp.float32
        )
        * score_scale
    )
    row_top = jnp.maximum(band_top, jnp.max(jnp.where(vert_allowed, vert_scores, neg), axis=(3, 4)))
    vert_w = jnp.where(vert_allowed, jnp.exp(vert_scores - row_top[..., None, None]), 0.0)
    band_scale = jnp.exp(band_top - row_top)
    row_total = band_total * band_scale + jnp.sum(vert_w, axis=(3, 4))
    blended = band_out * band_scale[..., None] + jnp.einsum(
        "hbqvk,hvkd->hbqd",
        vert_w.astype(jnp.bfloat16),
        vert_v,
        preferred_element_type=jnp.float32,
    )
    attended = (blended / row_total[..., None]).astype(jnp.bfloat16)
    attended, weight_cols = lax.optimization_barrier((attended, weight_cols))
    cz_count = lax.axis_size("cz")
    tiles = attended.transpose(1, 2, 0, 3).reshape(block_count, TILE_TOKENS, per_dev * HEAD_SIZE)
    spread_tiles = jnp.broadcast_to(
        tiles[:, None], (block_count, cz_count) + tiles.shape[1:]
    ).reshape(block_count * cz_count, TILE_TOKENS, per_dev * HEAD_SIZE)
    got = lax.all_to_all(spread_tiles, HEAD_AXES + ("cz",), split_axis=0, concat_axis=0, tiled=True)
    attn_group = got.reshape(head_count, cz_count, TILE_TOKENS, per_dev * HEAD_SIZE)
    projected = jnp.einsum(
        "hztd,hdn->ztn",
        attn_group,
        weight_cols.reshape(head_count, per_dev * HEAD_SIZE, -1),
        preferred_element_type=jnp.float32,
    ).astype(jnp.bfloat16).reshape(cz_count * TILE_TOKENS, -1)
    return lax.all_to_all(projected, "cz", split_axis=0, concat_axis=1, tiled=True)


def solution(mesh):
    ctx_count = mesh.shape["ctx"]
    cx_count = 4 if ctx_count % 4 == 0 else 1
    head_total = mesh.shape["head"]
    split_mesh = Mesh(
        mesh.devices.reshape(ctx_count // cx_count, cx_count, head_total // 2, 2),
        ("cz", "cx") + HEAD_AXES,
    )
    rows = P(("cz", "cx") + HEAD_AXES, None)
    placed = (rows, rows, rows, P(None, ("cz", "cx")), P(), P())
    return jax.shard_map(
        shards, mesh=split_mesh, in_specs=placed, out_specs=rows, check_vma=False
    )
```
